128 devices in a mesh: ctx: 16 (over x, y_hi, core), head: 8 (over z, y_lo).
Axes of the slice: x: 4, y: 4 (y_hi: 2, y_lo: 2; y = y_hi * 2 + y_lo), z: 4, core: 2. Of those that a mesh axis runs over, the one named last changes fastest.
Arguments:
- activations: bfloat16 [8192, 4096], P('ctx')
- qkv_weight: bfloat16 [4096, 3, 32, 128], P(None, None, 'head'), may hold values from -0.09375 to 0.09375
- out_weight: bfloat16 [32, 128, 4096], P('head'), may hold values from -0.09375 to 0.09375
- mod_table: float32 [16, 4096], replicated, may hold values from -3 to 3
- clip_level: int32 [64], replicated, may hold values from 0 to 15
- clip_of: int32 [8192], P('ctx'), may hold values from 0 to 63, never falling along the last dimension, each value on 1 to 256 neighbouring positions
- visible: int32 [64, 64], replicated, may hold values from 0 to 1, as said below
Outputs:
- mixed: bfloat16 [8192, 4096], P(('ctx', 'head'))
The draws below stay inside these ranges and needn't reach their ends.
Inputs may be any that keep to these rules, and one draw needn't show every extreme that they name: visible is 1 on the diagonal and 0 above it. `clip_of`: clip numbers never fall along the tokens; every clip has 1 to 256 tokens and one has exactly 256.
All inputs are finite; a program needn't handle non-finite values.
Results may differ from the reference program's by a relative error of at most 0.02.
The reference program's roundings to bfloat16 on the way count: a program that leaves them out, or rounds other values in their place, can miss the bound.
Values may be sent and summed in bfloat16 or wider, within the bound.
No kernel may reach another device: no remote copies, remote signals or barrier semaphores. Data moves between devices by JAX's collectives and lax.ppermute only.
A program may use at most 128 MiB of HBM per device.

```python
import math
import jax
import jax.numpy as jnp
import numpy as np
from jax import lax

D = 4096
HEADS = 32
HDIM = 128
TOKENS = 8192
CLIPS = 64
CLIP_MOST = 256
LEVELS = 16


def draw_activations(key, part):
    first_key = jax.random.fold_in(key, 0)
    values = jax.random.normal(first_key, (TOKENS, D), jnp.float32)
    return values.astype(jnp.bfloat16)


def draw_visible(key, part):
    draws = jax.random.randint(key, (CLIPS, CLIPS), 0, 4)
    row_ids = lax.broadcasted_iota(jnp.int32, (CLIPS, CLIPS), 0)
    col_ids = lax.broadcasted_iota(jnp.int32, (CLIPS, CLIPS), 1)
    below = jnp.where(draws > 0, 1, 0)
    return jnp.where(col_ids == row_ids, 1, jnp.where(col_ids < row_ids, below, 0)).astype(jnp.int32)


def place_ends(array, rng, least, largest):
    dims = array.shape
    index_at = [jax.random.randint(jax.random.fold_in(rng, axis), (), 0, dims[axis]) for axis in range(len(dims))]
    array = array.at[tuple(index_at)].set(least)
    longest = dims.index(max(dims))
    index_at[longest] = (index_at[longest] + 1) % dims[longest]
    return array.at[tuple(index_at)].set(largest)


def steps_of(key, dims, shards, least, top_value):
    level, own = 1.0, jax.random.fold_in(key, 6)
    for axis_at, parts in shards:
        heights = jnp.exp(jax.random.uniform(jax.random.fold_in(own, axis_at), (parts,), jnp.float32, least / len(shards), top_value / len(shards)))
        level = level * jnp.repeat(heights, dims[axis_at] // parts).reshape([-1 if axis == axis_at else 1 for axis in range(len(dims))])
    return level


def split_up(count, total, limit, skew):
    loads = [(1 << 20) // math.isqrt(standing ** skew) + 1 for standing in range(2, count + 1)]
    spare, counts = total - limit - (count - 1), [1] * (count - 1)
    while spare > 0:
        movable = [i for i in range(count - 1) if counts[i] < limit]
        whole, left = sum([loads[i] for i in movable]), spare
        for i in movable:
            extra = min(limit - counts[i], max(1, left * loads[i] // whole), spare)
            counts[i] = counts[i] + extra
            spare = spare - extra
    return np.array([limit] + counts)


def uneven_parts(stream_key, count, total, limit, lean):
    if count == 2:
        one = jax.random.randint(stream_key, (), max(1, total - limit), min(limit, total - 1) + 1)
        return jnp.stack([one, total - one])
    sizes = jnp.asarray(split_up(count, total, limit, lean), jnp.int32)
    pairs = (count - 1) // 2
    source_of, sink = sizes[1:1 + 2 * pairs:2], sizes[2:2 + 2 * pairs:2]
    room = jnp.minimum(source_of - 1, limit - sink)
    shifted = jax.random.randint(jax.random.fold_in(stream_key, 1), (pairs,), 0, 1 << 20) % (room + 1)
    sizes = sizes.at[1:1 + 2 * pairs:2].set(source_of - shifted).at[2:2 + 2 * pairs:2].set(sink + shifted)
    return sizes[jax.random.permutation(jax.random.fold_in(stream_key, 2), count)]


def noise(rng, extent, scale, reach, pieces=(), dtype=jnp.bfloat16):
    values = scale * jax.random.normal(rng, extent, jnp.float32)
    if pieces:
        values = values * steps_of(rng, extent, pieces, -0.22, 0.18)
    return jnp.clip(values, -reach, reach).astype(dtype)


def setup_inputs(seed: int = 0) -> dict:
    splits = jax.random.split(jax.random.key(seed), 8)
    return {
        "activations": draw_activations(jax.random.fold_in(splits[7], 71), 0),
        "qkv_weight": noise(splits[1], (D, 3, HEADS, HDIM), D ** -0.5, 0.09375, ((2, 8),)),
        "out_weight": noise(splits[2], (HEADS, HDIM, D), (HEADS * HDIM) ** -0.5, 0.09375, ((0, 8),)),
        "mod_table": noise(splits[3], (LEVELS, D), 0.4, 3.0, (), jnp.float32),
        "clip_level": place_ends(jax.random.randint(splits[4], (CLIPS,), 0, LEVELS), jax.random.fold_in(splits[4], 1), 0, LEVELS - 1).astype(jnp.int32),
        "clip_of": jnp.searchsorted(jnp.cumsum(uneven_parts(splits[5], CLIPS, TOKENS, CLIP_MOST, 2)), jnp.arange(TOKENS), side="right").astype(jnp.int32),
        "visible": draw_visible(jax.random.fold_in(splits[7], 71), 0),
    }


def reference(activations, qkv_weight, out_weight, mod_table, clip_level, clip_of, visible):
    level_tok = clip_level[clip_of]
    moduled = (activations.astype(jnp.float32) * (1.0 + mod_table[level_tok])).astype(jnp.bfloat16)
    qkv = jnp.einsum('td,dchk->tchk', moduled.astype(jnp.float32), qkv_weight.astype(jnp.float32)).astype(jnp.bfloat16)
    queries = qkv[:, 0]
    key_rows = qkv[:, 1]
    value_rows = qkv[:, 2]
    allowed = visible[clip_of][:, clip_of] > 0
    score_scale = 1.0 / jnp.sqrt(jnp.float32(HDIM))

    def single_head(head_index):
        q_head = queries[:, head_index]
        k_head = key_rows[:, head_index]
        v_head = value_rows[:, head_index]
        scores = jnp.dot(q_head, k_head.T, preferred_element_type=jnp.float32) * score_scale
        masked = jnp.where(allowed, scores, -jnp.inf)
        top_score = lax.optimization_barrier(jnp.max(masked, axis=1, keepdims=True))
        weights = jnp.where(allowed, jnp.exp(scores - top_score), 0.0)
        totals = lax.optimization_barrier(jnp.sum(weights, axis=1, keepdims=True))
        summed = jnp.dot(weights.astype(jnp.bfloat16), v_head, preferred_element_type=jnp.float32)
        return (summed / totals).astype(jnp.bfloat16)
    attended = lax.map(single_head, jnp.arange(HEADS))
    mixed = jnp.einsum('htd,hdo->to', attended.astype(jnp.float32), out_weight.astype(jnp.float32))
    return mixed.astype(jnp.bfloat16)
```

```python
import functools
import math

import jax
import numpy as np
import jax.numpy as jnp
from jax import lax
from jax.experimental import pallas as pl
from jax.experimental.pallas import tpu as pltpu
from jax.sharding import PartitionSpec as P


def attn_kernel(qvis_ref, q_ref, k_ref, v_ref, kh_ref, o_ref, m_sc, l_sc, acc_sc, bias_sc, *, scale, nsteps):
    j = pl.program_id(0)
    h = pl.program_id(1)

    @pl.when((j == 0) & (h == 0))
    def _():
        m_sc[...] = jnp.full(m_sc.shape, -1e30, jnp.float32)
        l_sc[...] = jnp.zeros(l_sc.shape, jnp.float32)
        acc_sc[...] = jnp.zeros(acc_sc.shape, jnp.float32)

    @pl.when(h == 0)
    def _():
        allowed = jnp.dot(qvis_ref[...], kh_ref[...], preferred_element_type=jnp.float32)
        bias_sc[...] = jnp.where(allowed > 0.5, 0.0, -jnp.inf).astype(jnp.float32)

    q = q_ref[h]
    k = k_ref[...]
    v = v_ref[...]
    s = lax.dot_general(q, k, (((1,), (1,)), ((), ())), preferred_element_type=jnp.float32)
    s = s * scale + bias_sc[...]
    m_old = m_sc[h]
    m_new = jnp.maximum(m_old, jnp.max(s, axis=1, keepdims=True))
    p = jnp.exp(s - m_new)
    alpha = jnp.exp(m_old - m_new)
    l_sc[h] = l_sc[h] * alpha + jnp.sum(p, axis=1, keepdims=True)
    acc_sc[h] = acc_sc[h] * alpha + jnp.dot(p.astype(jnp.bfloat16), v, preferred_element_type=jnp.float32)
    m_sc[h] = m_new

    @pl.when(j == nsteps - 1)
    def _():
        out = (acc_sc[h] / l_sc[h]).astype(o_ref.dtype)
        col = pl.multiple_of(h * q_ref.shape[2], q_ref.shape[2])
        o_ref[:, pl.ds(col, q_ref.shape[2])] = out


def flash_attention(qvis, q, kv_all, key_hot, scale):
    heads, nq, hd = q.shape
    sources, _, _, tok, _ = kv_all.shape
    clip_count = qvis.shape[1]
    bk = math.gcd(tok, 512)
    sub = tok // bk
    nsteps = sources * sub
    kernel = functools.partial(attn_kernel, scale=scale, nsteps=nsteps)
    flops = 4 * heads * nq * sources * tok * hd + 2 * nq * clip_count * sources * tok
    cost = pl.CostEstimate(
        flops=flops,
        transcendentals=heads * nq * sources * tok,
        bytes_accessed=kv_all.size * 2 + q.size * 2 + nq * heads * hd * 2,
    )
    return pl.pallas_call(
        kernel,
        grid=(nsteps, heads),
        in_specs=[
            pl.BlockSpec((nq, clip_count), lambda j, h: (0, 0)),
            pl.BlockSpec((heads, nq, hd), lambda j, h: (0, 0, 0)),
            pl.BlockSpec((None, None, None, bk, hd), lambda j, h: (j // sub, 0, h, j % sub, 0)),
            pl.BlockSpec((None, None, None, bk, hd), lambda j, h: (j // sub, 1, h, j % sub, 0)),
            pl.BlockSpec((None, clip_count, bk), lambda j, h: (j // sub, 0, j % sub)),
        ],
        out_specs=pl.BlockSpec((nq, heads * hd), lambda j, h: (0, 0)),
        out_shape=jax.ShapeDtypeStruct((nq, heads * hd), jnp.bfloat16),
        scratch_shapes=[
            pltpu.VMEM((heads, nq, 1), jnp.float32),
            pltpu.VMEM((heads, nq, 1), jnp.float32),
            pltpu.VMEM((heads, nq, hd), jnp.float32),
            pltpu.VMEM((nq, bk), jnp.float32),
        ],
        compiler_params=pltpu.CompilerParams(dimension_semantics=("arbitrary", "arbitrary")),
        cost_estimate=cost,
    )(qvis, q, kv_all, kv_all, key_hot)


def per_device(activations, qkv_weight, out_weight, mod_table, clip_level, clip_of, visible):
    heads_here = qkv_weight.shape[2]
    head_size = qkv_weight.shape[3]
    clip_count = visible.shape[0]
    level_count = mod_table.shape[0]
    clip_ids = lax.broadcasted_iota(jnp.int32, (1, clip_count), 1)
    level_ids = lax.broadcasted_iota(jnp.int32, (1, level_count), 1)
    tok_hot = clip_of[:, None] == clip_ids
    level_rows = jnp.sum(jnp.where(tok_hot, clip_level[None, :], 0), axis=1)
    level_hot = (level_rows[:, None] == level_ids).astype(jnp.float32)
    modulation = jnp.dot(level_hot, mod_table, precision=lax.Precision.HIGHEST)
    moduled = (activations.astype(jnp.float32) * (1.0 + modulation)).astype(jnp.bfloat16)
    qkv = jnp.einsum(
        "td,dchk->chtk", moduled, qkv_weight, preferred_element_type=jnp.float32
    ).astype(jnp.bfloat16)
    queries = qkv[0]
    kv_local = qkv[1:3]
    query_hot = tok_hot.astype(jnp.float32)
    qvis = jnp.dot(query_hot, visible.astype(jnp.float32), precision=lax.Precision.HIGHEST).astype(jnp.bfloat16)
    score_scale = float(np.float32(1.0) / np.sqrt(np.float32(head_size)))
    kv_all = lax.all_gather(kv_local, "ctx", axis=0)
    clips_all = lax.all_gather(clip_of, "ctx", axis=0)
    key_hot = (clips_all[:, None, :] == clip_ids[0][None, :, None]).astype(jnp.bfloat16)
    attended = flash_attention(qvis, queries, kv_all, key_hot, score_scale)
    ow = out_weight.reshape(heads_here * head_size, out_weight.shape[2])
    mixed = jnp.dot(attended, ow, preferred_element_type=jnp.float32).astype(jnp.bfloat16)
    return lax.psum_scatter(mixed, "head", scatter_dimension=0, tiled=True)


def solution(mesh):
    placed = (
        P("ctx", None),
        P(None, None, "head", None),
        P("head", None, None),
        P(),
        P(),
        P("ctx"),
        P(),
    )
    return jax.shard_map(
        per_device, mesh=mesh, in_specs=placed, out_specs=P(("ctx", "head"), None), check_vma=False
    )
```

```python
import functools
import math

import jax
import numpy as np
import jax.numpy as jnp
from jax import lax
from jax.experimental import pallas as pl
from jax.experimental.pallas import tpu as pltpu
from jax.sharding import PartitionSpec as P


def attn_kernel(qvis_ref, q_ref, k_ref, v_ref, kh_ref, o_ref, m_sc, l_sc, acc_sc, bias_sc, *, scale, nsteps):
    j = pl.program_id(0)
    h = pl.program_id(1)

    @pl.when((j == 0) & (h == 0))
    def _():
        m_sc[...] = jnp.full(m_sc.shape, -1e30, jnp.float32)
        l_sc[...] = jnp.zeros(l_sc.shape, jnp.float32)
        acc_sc[...] = jnp.zeros(acc_sc.shape, jnp.float32)

    @pl.when(h == 0)
    def _():
        allowed = jnp.dot(qvis_ref[...], kh_ref[...], preferred_element_type=jnp.float32)
        bias_sc[...] = jnp.where(allowed > 0.5, 0.0, -jnp.inf).astype(jnp.float32)

    q = q_ref[h]
    k = k_ref[...]
    v = v_ref[...]
    s = lax.dot_general(q, k, (((1,), (1,)), ((), ())), preferred_element_type=jnp.float32)
    s = s * scale + bias_sc[...]
    m_old = m_sc[h]
    m_new = jnp.maximum(m_old, jnp.max(s, axis=1, keepdims=True))
    p = jnp.exp(s - m_new)
    alpha = jnp.exp(m_old - m_new)
    l_sc[h] = l_sc[h] * alpha + jnp.sum(p, axis=1, keepdims=True)
    acc_sc[h] = acc_sc[h] * alpha + jnp.dot(p.astype(jnp.bfloat16), v, preferred_element_type=jnp.float32)
    m_sc[h] = m_new

    @pl.when(j == nsteps - 1)
    def _():
        out = (acc_sc[h] / l_sc[h]).astype(o_ref.dtype)
        col = pl.multiple_of(h * q_ref.shape[2], q_ref.shape[2])
        o_ref[:, pl.ds(col, q_ref.shape[2])] = out


def flash_attention(qvis, q, kv_all, key_hot, scale):
    heads, nq, hd = q.shape
    sources, _, _, tok, _ = kv_all.shape
    clip_count = qvis.shape[1]
    bk = math.gcd(tok, 512)
    sub = tok // bk
    nsteps = sources * sub
    kernel = functools.partial(attn_kernel, scale=scale, nsteps=nsteps)
    flops = 4 * heads * nq * sources * tok * hd + 2 * nq * clip_count * sources * tok
    cost = pl.CostEstimate(
        flops=flops,
        transcendentals=heads * nq * sources * tok,
        bytes_accessed=kv_all.size * 2 + q.size * 2 + nq * heads * hd * 2,
    )
    return pl.pallas_call(
        kernel,
        grid=(nsteps, heads),
        in_specs=[
            pl.BlockSpec((nq, clip_count), lambda j, h: (0, 0)),
            pl.BlockSpec((heads, nq, hd), lambda j, h: (0, 0, 0)),
            pl.BlockSpec((None, None, None, bk, hd), lambda j, h: (j // sub, 0, h, j % sub, 0)),
            pl.BlockSpec((None, None, None, bk, hd), lambda j, h: (j // sub, 1, h, j % sub, 0)),
            pl.BlockSpec((None, clip_count, bk), lambda j, h: (j // sub, 0, j % sub)),
        ],
        out_specs=pl.BlockSpec((nq, heads * hd), lambda j, h: (0, 0)),
        out_shape=jax.ShapeDtypeStruct((nq, heads * hd), jnp.bfloat16),
        scratch_shapes=[
            pltpu.VMEM((heads, nq, 1), jnp.float32),
            pltpu.VMEM((heads, nq, 1), jnp.float32),
            pltpu.VMEM((heads, nq, hd), jnp.float32),
            pltpu.VMEM((nq, bk), jnp.float32),
        ],
        compiler_params=pltpu.CompilerParams(dimension_semantics=("arbitrary", "arbitrary")),
        cost_estimate=cost,
    )(qvis, q, kv_all, kv_all, key_hot)


def per_device(activations, qkv_weight, out_weight, mod_table, clip_level, clip_of, visible):
    heads_here = qkv_weight.shape[2]
    head_size = qkv_weight.shape[3]
    clip_count = visible.shape[0]
    level_count = mod_table.shape[0]
    clip_ids = lax.broadcasted_iota(jnp.int32, (1, clip_count), 1)
    level_ids = lax.broadcasted_iota(jnp.int32, (1, level_count), 1)
    tok_hot = clip_of[:, None] == clip_ids
    level_rows = jnp.sum(jnp.where(tok_hot, clip_level[None, :], 0), axis=1)
    level_hot = (level_rows[:, None] == level_ids).astype(jnp.float32)
    modulation = jnp.dot(level_hot, mod_table, precision=lax.Precision.HIGHEST)
    moduled = (activations.astype(jnp.float32) * (1.0 + modulation)).astype(jnp.bfloat16)
    qkv = jnp.einsum(
        "td,dchk->chtk", moduled, qkv_weight, preferred_element_type=jnp.float32
    ).astype(jnp.bfloat16)
    queries = qkv[0]
    kv_local = qkv[1:3]
    query_hot = tok_hot.astype(jnp.float32)
    qvis = jnp.dot(query_hot, visible.astype(jnp.float32), precision=lax.Precision.HIGHEST).astype(jnp.bfloat16)
    score_scale = float(np.float32(1.0) / np.sqrt(np.float32(head_size)))
    kv_all = lax.all_gather(kv_local, "ctx", axis=0)
    clips_all = lax.all_gather(clip_of, "ctx", axis=0)
    key_hot = (clips_all[:, None, :] == clip_ids[0][None, :, None]).astype(jnp.bfloat16)
    attended = flash_attention(qvis, queries, kv_all, key_hot, score_scale)
    ow = out_weight.reshape(heads_here * head_size, out_weight.shape[2])
    mixed = jnp.dot(attended, ow, preferred_element_type=jnp.float32).astype(jnp.bfloat16)
    groups = lax.axis_size("head")
    parts = mixed.reshape(groups, mixed.shape[0] // groups, mixed.shape[1])
    parts = lax.all_to_all(parts, "head", 0, 0)
    return jnp.sum(parts.astype(jnp.float32), axis=0).astype(jnp.bfloat16)


def solution(mesh):
    placed = (
        P("ctx", None),
        P(None, None, "head", None),
        P("head", None, None),
        P(),
        P(),
        P("ctx"),
        P(),
    )
    return jax.shard_map(
        per_device, mesh=mesh, in_specs=placed, out_specs=P(("ctx", "head"), None), check_vma=False
    )
```

```python
import functools
import math

import jax
import numpy as np
import jax.numpy as jnp
from jax import lax
from jax.experimental import pallas as pl
from jax.experimental.pallas import tpu as pltpu
from jax.sharding import PartitionSpec as P


def attn_kernel(qvis_ref, q_ref, kv_ref, kh_ref, o_ref, m_sc, l_sc, acc_sc, *, scale, nsteps, heads):
    j = pl.program_id(0)
    lanes = m_sc.shape[2]

    @pl.when(j == 0)
    def _():
        m_sc[...] = jnp.full(m_sc.shape, -1e30, jnp.float32)
        l_sc[...] = jnp.zeros(l_sc.shape, jnp.float32)
        acc_sc[...] = jnp.zeros(acc_sc.shape, jnp.float32)

    allowed = jnp.dot(qvis_ref[...], kh_ref[...], preferred_element_type=jnp.float32)
    bias = jnp.where(allowed > 0.5, 0.0, -jnp.inf).astype(jnp.float32)
    bk = bias.shape[1]
    for h in range(heads):
        s = lax.dot_general(q_ref[h], kv_ref[0, h], (((1,), (1,)), ((), ())), preferred_element_type=jnp.float32)
        s = s * scale + bias
        m_old = m_sc[h]
        m_new = jnp.maximum(m_old, jnp.max(s, axis=1, keepdims=True))
        p = jnp.exp(s - jnp.tile(m_new, (1, bk // lanes)))
        alpha = jnp.exp(m_old - m_new)
        l_sc[h] = l_sc[h] * alpha + jnp.sum(p, axis=1, keepdims=True)
        acc_sc[h] = acc_sc[h] * alpha + jnp.dot(
            p.astype(jnp.bfloat16), kv_ref[1, h], preferred_element_type=jnp.float32
        )
        m_sc[h] = m_new

    @pl.when(j == nsteps - 1)
    def _():
        hd = acc_sc.shape[2]
        for h in range(heads):
            o_ref[:, h * hd:(h + 1) * hd] = (acc_sc[h] / l_sc[h]).astype(o_ref.dtype)


def flash_attention(qvis, q, kv_all, key_hot, scale):
    heads, nq, hd = q.shape
    sources, _, _, tok, _ = kv_all.shape
    clip_count = qvis.shape[1]
    bk = math.gcd(tok, 512)
    sub = tok // bk
    nsteps = sources * sub
    kernel = functools.partial(attn_kernel, scale=scale, nsteps=nsteps, heads=heads)
    flops = 4 * heads * nq * sources * tok * hd + 2 * nq * clip_count * sources * tok
    cost = pl.CostEstimate(
        flops=flops,
        transcendentals=heads * nq * sources * tok,
        bytes_accessed=kv_all.size * 2 + q.size * 2 + nq * heads * hd * 2,
    )
    return pl.pallas_call(
        kernel,
        grid=(nsteps,),
        in_specs=[
            pl.BlockSpec((nq, clip_count), lambda j: (0, 0)),
            pl.BlockSpec((heads, nq, hd), lambda j: (0, 0, 0)),
            pl.BlockSpec((None, 2, heads, bk, hd), lambda j: (j // sub, 0, 0, j % sub, 0)),
            pl.BlockSpec((None, clip_count, bk), lambda j: (j // sub, 0, j % sub)),
        ],
        out_specs=pl.BlockSpec((nq, heads * hd), lambda j: (0, 0)),
        out_shape=jax.ShapeDtypeStruct((nq, heads * hd), jnp.bfloat16),
        scratch_shapes=[
            pltpu.VMEM((heads, nq, 128), jnp.float32),
            pltpu.VMEM((heads, nq, 128), jnp.float32),
            pltpu.VMEM((heads, nq, hd), jnp.float32),
        ],
        compiler_params=pltpu.CompilerParams(dimension_semantics=("arbitrary",)),
        cost_estimate=cost,
    )(qvis, q, kv_all, key_hot)


def per_device(activations, qkv_weight, out_weight, mod_table, clip_level, clip_of, visible):
    heads_here = qkv_weight.shape[2]
    head_size = qkv_weight.shape[3]
    clip_count = visible.shape[0]
    level_count = mod_table.shape[0]
    clip_ids = lax.broadcasted_iota(jnp.int32, (1, clip_count), 1)
    level_ids = lax.broadcasted_iota(jnp.int32, (1, level_count), 1)
    tok_hot = clip_of[:, None] == clip_ids
    level_rows = jnp.sum(jnp.where(tok_hot, clip_level[None, :], 0), axis=1)
    level_hot = (level_rows[:, None] == level_ids).astype(jnp.float32)
    modulation = jnp.dot(level_hot, mod_table, precision=lax.Precision.HIGHEST)
    moduled = (activations.astype(jnp.float32) * (1.0 + modulation)).astype(jnp.bfloat16)
    qkv = jnp.einsum(
        "td,dchk->chtk", moduled, qkv_weight, preferred_element_type=jnp.float32
    ).astype(jnp.bfloat16)
    queries = qkv[0]
    kv_local = qkv[1:3]
    query_hot = tok_hot.astype(jnp.float32)
    qvis = jnp.dot(query_hot, visible.astype(jnp.float32), precision=lax.Precision.HIGHEST).astype(jnp.bfloat16)
    score_scale = float(np.float32(1.0) / np.sqrt(np.float32(head_size)))
    kv_all = lax.all_gather(kv_local, "ctx", axis=0)
    clips_all = lax.all_gather(clip_of, "ctx", axis=0)
    key_hot = (clips_all[:, None, :] == clip_ids[0][None, :, None]).astype(jnp.bfloat16)
    attended = flash_attention(qvis, queries, kv_all, key_hot, score_scale)
    ow = out_weight.reshape(heads_here * head_size, out_weight.shape[2])
    mixed = jnp.dot(attended, ow, preferred_element_type=jnp.float32).astype(jnp.bfloat16)
    groups = lax.axis_size("head")
    parts = mixed.reshape(groups, mixed.shape[0] // groups, mixed.shape[1])
    parts = lax.all_to_all(parts, "head", 0, 0)
    return jnp.sum(parts.astype(jnp.float32), axis=0).astype(jnp.bfloat16)


def solution(mesh):
    placed = (
        P("ctx", None),
        P(None, None, "head", None),
        P("head", None, None),
        P(),
        P(),
        P("ctx"),
        P(),
    )
    return jax.shard_map(
        per_device, mesh=mesh, in_specs=placed, out_specs=P(("ctx", "head"), None), check_vma=False
    )
```

```python
import functools
import math

import jax
import numpy as np
import jax.numpy as jnp
from jax import lax
from jax.experimental import pallas as pl
from jax.experimental.pallas import tpu as pltpu
from jax.sharding import Mesh, PartitionSpec as P


def attn_kernel(qvis_ref, q_ref, kv_ref, kh_ref, o_ref, m_sc, l_sc, acc_sc, *, scale, nsteps, heads):
    j = pl.program_id(0)
    lanes = m_sc.shape[2]

    @pl.when(j == 0)
    def _():
        m_sc[...] = jnp.full(m_sc.shape, -1e30, jnp.float32)
        l_sc[...] = jnp.zeros(l_sc.shape, jnp.float32)
        acc_sc[...] = jnp.zeros(acc_sc.shape, jnp.float32)

    allowed = jnp.dot(qvis_ref[...], kh_ref[...], preferred_element_type=jnp.float32)
    bias = jnp.where(allowed > 0.5, 0.0, -jnp.inf).astype(jnp.float32)
    bk = bias.shape[1]
    for h in range(heads):
        s = lax.dot_general(q_ref[h], kv_ref[0, h], (((1,), (1,)), ((), ())), preferred_element_type=jnp.float32)
        s = s * scale + bias
        m_old = m_sc[h]
        m_new = jnp.maximum(m_old, jnp.max(s, axis=1, keepdims=True))
        p = jnp.exp(s - jnp.tile(m_new, (1, bk // lanes)))
        alpha = jnp.exp(m_old - m_new)
        l_sc[h] = l_sc[h] * alpha + jnp.sum(p, axis=1, keepdims=True)
        acc_sc[h] = acc_sc[h] * alpha + jnp.dot(
            p.astype(jnp.bfloat16), kv_ref[1, h], preferred_element_type=jnp.float32
        )
        m_sc[h] = m_new

    @pl.when(j == nsteps - 1)
    def _():
        hd = acc_sc.shape[2]
        for h in range(heads):
            o_ref[:, h * hd:(h + 1) * hd] = (acc_sc[h] / l_sc[h]).astype(o_ref.dtype)


def flash_attention(qvis, q, kv_all, key_hot, scale):
    heads, nq, hd = q.shape
    sources, _, _, tok, _ = kv_all.shape
    clip_count = qvis.shape[1]
    bk = math.gcd(tok, 512)
    sub = tok // bk
    nsteps = sources * sub
    kernel = functools.partial(attn_kernel, scale=scale, nsteps=nsteps, heads=heads)
    flops = 4 * heads * nq * sources * tok * hd + 2 * nq * clip_count * sources * tok
    cost = pl.CostEstimate(
        flops=flops,
        transcendentals=heads * nq * sources * tok,
        bytes_accessed=kv_all.size * 2 + q.size * 2 + nq * heads * hd * 2,
    )
    return pl.pallas_call(
        kernel,
        grid=(nsteps,),
        in_specs=[
            pl.BlockSpec((nq, clip_count), lambda j: (0, 0)),
            pl.BlockSpec((heads, nq, hd), lambda j: (0, 0, 0)),
            pl.BlockSpec((None, 2, heads, bk, hd), lambda j: (j // sub, 0, 0, j % sub, 0)),
            pl.BlockSpec((None, clip_count, bk), lambda j: (j // sub, 0, j % sub)),
        ],
        out_specs=pl.BlockSpec((nq, heads * hd), lambda j: (0, 0)),
        out_shape=jax.ShapeDtypeStruct((nq, heads * hd), jnp.bfloat16),
        scratch_shapes=[
            pltpu.VMEM((heads, nq, 128), jnp.float32),
            pltpu.VMEM((heads, nq, 128), jnp.float32),
            pltpu.VMEM((heads, nq, hd), jnp.float32),
        ],
        compiler_params=pltpu.CompilerParams(dimension_semantics=("arbitrary",)),
        cost_estimate=cost,
    )(qvis, q, kv_all, key_hot)


def per_device(activations, qkv_weight, out_weight, mod_table, clip_level, clip_of, visible):
    heads_here = qkv_weight.shape[2]
    head_size = qkv_weight.shape[3]
    clip_count = visible.shape[0]
    level_count = mod_table.shape[0]
    clip_ids = lax.broadcasted_iota(jnp.int32, (1, clip_count), 1)
    level_ids = lax.broadcasted_iota(jnp.int32, (1, level_count), 1)
    tok_hot = clip_of[:, None] == clip_ids
    level_rows = jnp.sum(jnp.where(tok_hot, clip_level[None, :], 0), axis=1)
    level_hot = (level_rows[:, None] == level_ids).astype(jnp.float32)
    modulation = jnp.dot(level_hot, mod_table, precision=lax.Precision.HIGHEST)
    moduled = (activations.astype(jnp.float32) * (1.0 + modulation)).astype(jnp.bfloat16)
    qkv = jnp.einsum(
        "td,dchk->chtk", moduled, qkv_weight, preferred_element_type=jnp.float32
    ).astype(jnp.bfloat16)
    core = lax.axis_index("core")
    half = heads_here // 2
    swap = [(0, 1), (1, 0)]
    mine = lax.dynamic_slice_in_dim(qkv, core * half, half, axis=1)
    other = lax.dynamic_slice_in_dim(qkv, (1 - core) * half, half, axis=1)
    recv = lax.ppermute(other, "core", swap)
    clip_recv = lax.ppermute(clip_of, "core", swap)
    both = jnp.concatenate([mine, recv], axis=2)
    clip_pair = jnp.concatenate([clip_of, clip_recv])
    queries = both[0]
    kv_local = both[1:3]
    pair_hot = (clip_pair[:, None] == clip_ids).astype(jnp.float32)
    qvis = jnp.dot(pair_hot, visible.astype(jnp.float32), precision=lax.Precision.HIGHEST).astype(jnp.bfloat16)
    score_scale = float(np.float32(1.0) / np.sqrt(np.float32(head_size)))
    kv_all = lax.all_gather(kv_local, "cx", axis=0)
    clips_all = lax.all_gather(clip_pair, "cx", axis=0)
    key_hot = (clips_all[:, None, :] == clip_ids[0][None, :, None]).astype(jnp.bfloat16)
    attended = flash_attention(qvis, queries, kv_all, key_hot, score_scale)
    tok = clip_of.shape[0]
    att_back = lax.ppermute(attended[tok:], "core", swap)
    ow = out_weight.reshape(heads_here * head_size, out_weight.shape[2])
    ow_mine = lax.dynamic_slice_in_dim(ow, core * half * head_size, half * head_size, axis=0)
    ow_other = lax.dynamic_slice_in_dim(ow, (1 - core) * half * head_size, half * head_size, axis=0)
    mixed = (
        jnp.dot(attended[:tok], ow_mine, preferred_element_type=jnp.float32)
        + jnp.dot(att_back, ow_other, preferred_element_type=jnp.float32)
    ).astype(jnp.bfloat16)
    groups = lax.axis_size("head")
    parts = mixed.reshape(groups, mixed.shape[0] // groups, mixed.shape[1])
    parts = lax.all_to_all(parts, "head", 0, 0)
    return jnp.sum(parts.astype(jnp.float32), axis=0).astype(jnp.bfloat16)


def solution(mesh):
    ctx = mesh.shape["ctx"]
    fine = Mesh(mesh.devices.reshape(ctx // 2, 2, mesh.shape["head"]), ("cx", "core", "head"))
    placed = (
        P(("cx", "core"), None),
        P(None, None, "head", None),
        P("head", None, None),
        P(),
        P(),
        P(("cx", "core")),
        P(),
    )
    return jax.shard_map(
        per_device, mesh=fine, in_specs=placed, out_specs=P(("cx", "core", "head"), None), check_vma=False
    )
```

```python
import functools
import math

import jax
import numpy as np
import jax.numpy as jnp
from jax import lax
from jax.experimental import pallas as pl
from jax.experimental.pallas import tpu as pltpu
from jax.sharding import Mesh, PartitionSpec as P


def attn_kernel(qvis_ref, q_ref, kv_ref, kh_ref, o_ref, m_sc, l_sc, acc_sc, *, scale, nsteps, heads):
    j = pl.program_id(0)
    lanes = m_sc.shape[2]

    @pl.when(j == 0)
    def _():
        m_sc[...] = jnp.full(m_sc.shape, -1e30, jnp.float32)
        l_sc[...] = jnp.zeros(l_sc.shape, jnp.float32)
        acc_sc[...] = jnp.zeros(acc_sc.shape, jnp.float32)

    allowed = jnp.dot(qvis_ref[...], kh_ref[...], preferred_element_type=jnp.float32)
    bias = jnp.where(allowed > 0.5, 0.0, -jnp.inf).astype(jnp.float32)
    bk = bias.shape[1]
    for h in range(heads):
        s = lax.dot_general(q_ref[h], kv_ref[0, h], (((1,), (1,)), ((), ())), preferred_element_type=jnp.float32)
        s = s * scale + bias
        m_old = m_sc[h]
        m_new = jnp.maximum(m_old, jnp.max(s, axis=1, keepdims=True))
        p = jnp.exp(s - jnp.tile(m_new, (1, bk // lanes)))
        alpha = jnp.exp(m_old - m_new)
        l_sc[h] = l_sc[h] * alpha + jnp.sum(p, axis=1, keepdims=True)
        acc_sc[h] = acc_sc[h] * alpha + jnp.dot(
            p.astype(jnp.bfloat16), kv_ref[1, h], preferred_element_type=jnp.float32
        )
        m_sc[h] = m_new

    @pl.when(j == nsteps - 1)
    def _():
        hd = acc_sc.shape[2]
        for h in range(heads):
            o_ref[:, h * hd:(h + 1) * hd] = (acc_sc[h] / l_sc[h]).astype(o_ref.dtype)


def flash_attention(qvis, q, kv_all, key_hot, scale):
    heads, nq, hd = q.shape
    sources, _, _, tok, _ = kv_all.shape
    clip_count = qvis.shape[1]
    bk = math.gcd(tok, 512)
    sub = tok // bk
    nsteps = sources * sub
    kernel = functools.partial(attn_kernel, scale=scale, nsteps=nsteps, heads=heads)
    flops = 4 * heads * nq * sources * tok * hd + 2 * nq * clip_count * sources * tok
    cost = pl.CostEstimate(
        flops=flops,
        transcendentals=heads * nq * sources * tok,
        bytes_accessed=kv_all.size * 2 + q.size * 2 + nq * heads * hd * 2,
    )
    return pl.pallas_call(
        kernel,
        grid=(nsteps,),
        in_specs=[
            pl.BlockSpec((nq, clip_count), lambda j: (0, 0)),
            pl.BlockSpec((heads, nq, hd), lambda j: (0, 0, 0)),
            pl.BlockSpec((None, 2, heads, bk, hd), lambda j: (j // sub, 0, 0, j % sub, 0)),
            pl.BlockSpec((None, clip_count, bk), lambda j: (j // sub, 0, j % sub)),
        ],
        out_specs=pl.BlockSpec((nq, heads * hd), lambda j: (0, 0)),
        out_shape=jax.ShapeDtypeStruct((nq, heads * hd), jnp.bfloat16),
        scratch_shapes=[
            pltpu.VMEM((heads, nq, 128), jnp.float32),
            pltpu.VMEM((heads, nq, 128), jnp.float32),
            pltpu.VMEM((heads, nq, hd), jnp.float32),
        ],
        compiler_params=pltpu.CompilerParams(dimension_semantics=("arbitrary",)),
        cost_estimate=cost,
    )(qvis, q, kv_all, key_hot)


def attn_kernel1(qvis_ref, q_ref, k_ref, v_ref, kh_ref, o_ref, m_sc, l_sc, acc_sc, *, scale, nsteps):
    j = pl.program_id(0)
    lanes = m_sc.shape[1]

    @pl.when(j == 0)
    def _():
        m_sc[...] = jnp.full(m_sc.shape, -1e30, jnp.float32)
        l_sc[...] = jnp.zeros(l_sc.shape, jnp.float32)
        acc_sc[...] = jnp.zeros(acc_sc.shape, jnp.float32)

    allowed = jnp.dot(qvis_ref[...], kh_ref[...], preferred_element_type=jnp.float32)
    bias = jnp.where(allowed > 0.5, 0.0, -jnp.inf).astype(jnp.float32)
    bk = bias.shape[1]
    s = lax.dot_general(q_ref[...], k_ref[...], (((1,), (1,)), ((), ())), preferred_element_type=jnp.float32)
    s = s * scale + bias
    m_old = m_sc[...]
    m_new = jnp.maximum(m_old, jnp.max(s, axis=1, keepdims=True))
    p = jnp.exp(s - jnp.tile(m_new, (1, bk // lanes)))
    alpha = jnp.exp(m_old - m_new)
    l_sc[...] = l_sc[...] * alpha + jnp.sum(p, axis=1, keepdims=True)
    acc_sc[...] = acc_sc[...] * alpha + jnp.dot(
        p.astype(jnp.bfloat16), v_ref[...], preferred_element_type=jnp.float32
    )
    m_sc[...] = m_new

    @pl.when(j == nsteps - 1)
    def _():
        o_ref[...] = (acc_sc[...] / l_sc[...]).astype(o_ref.dtype)


def flash_attention1(qvis, q, kv_all, key_hot, scale, tok):
    nq, hd = q.shape
    sources = kv_all.shape[0]
    clip_count = qvis.shape[1]
    bk = math.gcd(tok, 512)
    sub = tok // bk
    nsteps = sources * sub
    kernel = functools.partial(attn_kernel1, scale=scale, nsteps=nsteps)
    cost = pl.CostEstimate(
        flops=4 * nq * sources * tok * hd + 2 * nq * clip_count * sources * tok,
        transcendentals=nq * sources * tok,
        bytes_accessed=kv_all.size * 2 + q.size * 4,
    )
    return pl.pallas_call(
        kernel,
        grid=(nsteps,),
        in_specs=[
            pl.BlockSpec((nq, clip_count), lambda j: (0, 0)),
            pl.BlockSpec((nq, hd), lambda j: (0, 0)),
            pl.BlockSpec((None, bk, hd), lambda j: (j // sub, j % sub, 0)),
            pl.BlockSpec((None, bk, hd), lambda j: (j // sub, sub + j % sub, 0)),
            pl.BlockSpec((None, clip_count, bk), lambda j: (j // sub, 0, j % sub)),
        ],
        out_specs=pl.BlockSpec((nq, hd), lambda j: (0, 0)),
        out_shape=jax.ShapeDtypeStruct((nq, hd), jnp.bfloat16),
        scratch_shapes=[
            pltpu.VMEM((nq, 128), jnp.float32),
            pltpu.VMEM((nq, 128), jnp.float32),
            pltpu.VMEM((nq, hd), jnp.float32),
        ],
        compiler_params=pltpu.CompilerParams(dimension_semantics=("arbitrary",)),
        cost_estimate=cost,
    )(qvis, q, kv_all, kv_all, key_hot)


def per_device(activations, qkv_weight, out_weight, mod_table, clip_level, clip_of, visible):
    heads_here = qkv_weight.shape[2]
    head_size = qkv_weight.shape[3]
    clip_count = visible.shape[0]
    level_count = mod_table.shape[0]
    tok = clip_of.shape[0]
    clip_ids = lax.broadcasted_iota(jnp.int32, (1, clip_count), 1)
    level_ids = lax.broadcasted_iota(jnp.int32, (1, level_count), 1)
    tok_hot = clip_of[:, None] == clip_ids
    level_rows = jnp.sum(jnp.where(tok_hot, clip_level[None, :], 0), axis=1)
    level_hot = (level_rows[:, None] == level_ids).astype(jnp.float32)
    modulation = jnp.dot(level_hot, mod_table, precision=lax.Precision.HIGHEST)
    moduled = (activations.astype(jnp.float32) * (1.0 + modulation)).astype(jnp.bfloat16)
    qkv = jnp.einsum(
        "td,dchk->hctk", moduled, qkv_weight, preferred_element_type=jnp.float32
    ).astype(jnp.bfloat16)
    lane = head_size
    clip_rows = tok // lane
    pad_rows = -clip_rows % 8
    clip_slab = jnp.concatenate(
        [clip_of.astype(jnp.bfloat16).reshape(clip_rows, lane), jnp.zeros((pad_rows, lane), jnp.bfloat16)]
    )
    payload = jnp.concatenate(
        [qkv.reshape(heads_here, 3 * tok, lane), jnp.broadcast_to(clip_slab, (heads_here,) + clip_slab.shape)],
        axis=1,
    )
    exch = lax.all_to_all(payload, "yc", 0, 0, tiled=True)
    group_tok = heads_here * tok
    queries = exch[:, 0:tok].reshape(group_tok, lane)
    keys = exch[:, tok:2 * tok].reshape(group_tok, lane)
    values = exch[:, 2 * tok:3 * tok].reshape(group_tok, lane)
    clip_group = exch[:, 3 * tok:3 * tok + clip_rows].reshape(group_tok)
    group_rows = group_tok // lane
    kv_pad = -group_rows % 8
    kv_payload = jnp.concatenate(
        [keys, values, clip_group.reshape(group_rows, lane), jnp.zeros((kv_pad, lane), jnp.bfloat16)]
    )
    kv_all = lax.all_gather(kv_payload, "x", axis=0)
    key_clips = kv_all[:, 2 * group_tok:2 * group_tok + group_rows].reshape(kv_all.shape[0], group_tok)
    key_hot = (key_clips.astype(jnp.int32)[:, None, :] == clip_ids[0][None, :, None]).astype(jnp.bfloat16)
    query_hot = (clip_group.astype(jnp.int32)[:, None] == clip_ids).astype(jnp.float32)
    qvis = jnp.dot(query_hot, visible.astype(jnp.float32), precision=lax.Precision.HIGHEST).astype(jnp.bfloat16)
    score_scale = float(np.float32(1.0) / np.sqrt(np.float32(head_size)))
    attended = flash_attention1(qvis, queries, kv_all, key_hot, score_scale, group_tok)
    back = lax.all_to_all(attended.reshape(heads_here, tok, lane), "yc", 0, 0, tiled=True)
    mixed = jnp.einsum(
        "hrd,hdo->ro", back, out_weight, preferred_element_type=jnp.float32
    ).astype(jnp.bfloat16)
    groups = lax.axis_size("head")
    parts = mixed.reshape(groups, mixed.shape[0] // groups, mixed.shape[1])
    parts = lax.all_to_all(parts, "head", 0, 0)
    return jnp.sum(parts.astype(jnp.float32), axis=0).astype(jnp.bfloat16)


def solution(mesh):
    ctx = mesh.shape["ctx"]
    heads = 4
    fine = Mesh(mesh.devices.reshape(ctx // heads, heads, mesh.shape["head"]), ("x", "yc", "head"))
    placed = (
        P(("x", "yc"), None),
        P(None, None, "head", None),
        P("head", None, None),
        P(),
        P(),
        P(("x", "yc")),
        P(),
    )
    return jax.shard_map(
        per_device, mesh=fine, in_specs=placed, out_specs=P(("x", "yc", "head"), None), check_vma=False
    )
```

```python
import functools
import math

import jax
import numpy as np
import jax.numpy as jnp
from jax import lax
from jax.experimental import pallas as pl
from jax.experimental.pallas import tpu as pltpu
from jax.sharding import Mesh, PartitionSpec as P


def attn_kernel(qvis_ref, q_ref, kv_ref, kh_ref, o_ref, m_sc, l_sc, acc_sc, *, scale, nsteps, heads):
    j = pl.program_id(0)
    lanes = m_sc.shape[2]

    @pl.when(j == 0)
    def _():
        m_sc[...] = jnp.full(m_sc.shape, -1e30, jnp.float32)
        l_sc[...] = jnp.zeros(l_sc.shape, jnp.float32)
        acc_sc[...] = jnp.zeros(acc_sc.shape, jnp.float32)

    allowed = jnp.dot(qvis_ref[...], kh_ref[...], preferred_element_type=jnp.float32)
    bias = jnp.where(allowed > 0.5, 0.0, -jnp.inf).astype(jnp.float32)
    bk = bias.shape[1]
    for h in range(heads):
        s = lax.dot_general(q_ref[h], kv_ref[0, h], (((1,), (1,)), ((), ())), preferred_element_type=jnp.float32)
        s = s * scale + bias
        m_old = m_sc[h]
        m_new = jnp.maximum(m_old, jnp.max(s, axis=1, keepdims=True))
        p = jnp.exp(s - jnp.tile(m_new, (1, bk // lanes)))
        alpha = jnp.exp(m_old - m_new)
        l_sc[h] = l_sc[h] * alpha + jnp.sum(p, axis=1, keepdims=True)
        acc_sc[h] = acc_sc[h] * alpha + jnp.dot(
            p.astype(jnp.bfloat16), kv_ref[1, h], preferred_element_type=jnp.float32
        )
        m_sc[h] = m_new

    @pl.when(j == nsteps - 1)
    def _():
        hd = acc_sc.shape[2]
        for h in range(heads):
            o_ref[:, h * hd:(h + 1) * hd] = (acc_sc[h] / l_sc[h]).astype(o_ref.dtype)


def flash_attention(qvis, q, kv_all, key_hot, scale):
    heads, nq, hd = q.shape
    sources, _, _, tok, _ = kv_all.shape
    clip_count = qvis.shape[1]
    bk = math.gcd(tok, 512)
    sub = tok // bk
    nsteps = sources * sub
    kernel = functools.partial(attn_kernel, scale=scale, nsteps=nsteps, heads=heads)
    flops = 4 * heads * nq * sources * tok * hd + 2 * nq * clip_count * sources * tok
    cost = pl.CostEstimate(
        flops=flops,
        transcendentals=heads * nq * sources * tok,
        bytes_accessed=kv_all.size * 2 + q.size * 2 + nq * heads * hd * 2,
    )
    return pl.pallas_call(
        kernel,
        grid=(nsteps,),
        in_specs=[
            pl.BlockSpec((nq, clip_count), lambda j: (0, 0)),
            pl.BlockSpec((heads, nq, hd), lambda j: (0, 0, 0)),
            pl.BlockSpec((None, 2, heads, bk, hd), lambda j: (j // sub, 0, 0, j % sub, 0)),
            pl.BlockSpec((None, clip_count, bk), lambda j: (j // sub, 0, j % sub)),
        ],
        out_specs=pl.BlockSpec((nq, heads * hd), lambda j: (0, 0)),
        out_shape=jax.ShapeDtypeStruct((nq, heads * hd), jnp.bfloat16),
        scratch_shapes=[
            pltpu.VMEM((heads, nq, 128), jnp.float32),
            pltpu.VMEM((heads, nq, 128), jnp.float32),
            pltpu.VMEM((heads, nq, hd), jnp.float32),
        ],
        compiler_params=pltpu.CompilerParams(dimension_semantics=("arbitrary",)),
        cost_estimate=cost,
    )(qvis, q, kv_all, key_hot)


def attn_kernel1(need_ref, qvis_ref, q_ref, k_ref, v_ref, kh_ref, o_ref, m_sc, l_sc, acc_sc, *, scale, nsteps, chunk):
    j = pl.program_id(0)
    lanes = m_sc.shape[1]

    @pl.when(j == 0)
    def _():
        m_sc[...] = jnp.full(m_sc.shape, -1e30, jnp.float32)
        l_sc[...] = jnp.zeros(l_sc.shape, jnp.float32)
        acc_sc[...] = jnp.zeros(acc_sc.shape, jnp.float32)

    for c in range(q_ref.shape[0] // chunk):
        rows = pl.ds(c * chunk, chunk)

        @pl.when(need_ref[c, j] > 0)
        def _():
            allowed = jnp.dot(qvis_ref[rows, :], kh_ref[...], preferred_element_type=jnp.float32)
            bias = jnp.where(allowed > 0.5, 0.0, -jnp.inf).astype(jnp.float32)
            bk = bias.shape[1]
            s = lax.dot_general(
                q_ref[rows, :], k_ref[...], (((1,), (1,)), ((), ())), preferred_element_type=jnp.float32
            )
            s = s * scale + bias
            m_old = m_sc[rows, :]
            m_new = jnp.maximum(m_old, jnp.max(s, axis=1, keepdims=True))
            p = jnp.exp(s - jnp.tile(m_new, (1, bk // lanes)))
            alpha = jnp.exp(m_old - m_new)
            l_sc[rows, :] = l_sc[rows, :] * alpha + jnp.sum(p, axis=1, keepdims=True)
            acc_sc[rows, :] = acc_sc[rows, :] * alpha + jnp.dot(
                p.astype(jnp.bfloat16), v_ref[...], preferred_element_type=jnp.float32
            )
            m_sc[rows, :] = m_new

    @pl.when(j == nsteps - 1)
    def _():
        o_ref[...] = (acc_sc[...] / l_sc[...]).astype(o_ref.dtype)


def flash_attention1(qvis, q, kv_all, key_hot, query_clips, key_clips, scale, tok):
    nq, hd = q.shape
    sources = kv_all.shape[0]
    clip_count = qvis.shape[1]
    bk = math.gcd(tok, 512)
    chunk = math.gcd(nq, 512)
    sub = tok // bk
    nsteps = sources * sub
    key_low = jnp.min(key_clips.reshape(nsteps, bk), axis=1)
    query_high = jnp.max(query_clips.reshape(nq // chunk, chunk), axis=1)
    need = (key_low[None, :] <= query_high[:, None]).astype(jnp.int32)
    kernel = functools.partial(attn_kernel1, scale=scale, nsteps=nsteps, chunk=chunk)
    cost = pl.CostEstimate(
        flops=4 * nq * sources * tok * hd + 2 * nq * clip_count * sources * tok,
        transcendentals=nq * sources * tok,
        bytes_accessed=kv_all.size * 2 + q.size * 4,
    )
    grid_spec = pltpu.PrefetchScalarGridSpec(
        num_scalar_prefetch=1,
        grid=(nsteps,),
        in_specs=[
            pl.BlockSpec((nq, clip_count), lambda j, n: (0, 0)),
            pl.BlockSpec((nq, hd), lambda j, n: (0, 0)),
            pl.BlockSpec((None, bk, hd), lambda j, n: (j // sub, j % sub, 0)),
            pl.BlockSpec((None, bk, hd), lambda j, n: (j // sub, sub + j % sub, 0)),
            pl.BlockSpec((None, clip_count, bk), lambda j, n: (j // sub, 0, j % sub)),
        ],
        out_specs=pl.BlockSpec((nq, hd), lambda j, n: (0, 0)),
        scratch_shapes=[
            pltpu.VMEM((nq, 128), jnp.float32),
            pltpu.VMEM((nq, 128), jnp.float32),
            pltpu.VMEM((nq, hd), jnp.float32),
        ],
    )
    return pl.pallas_call(
        kernel,
        grid_spec=grid_spec,
        out_shape=jax.ShapeDtypeStruct((nq, hd), jnp.bfloat16),
        compiler_params=pltpu.CompilerParams(dimension_semantics=("arbitrary",)),
        cost_estimate=cost,
    )(need, qvis, q, kv_all, kv_all, key_hot)


def per_device(activations, qkv_weight, out_weight, mod_table, clip_level, clip_of, visible):
    heads_here = qkv_weight.shape[2]
    head_size = qkv_weight.shape[3]
    clip_count = visible.shape[0]
    level_count = mod_table.shape[0]
    tok = clip_of.shape[0]
    clip_ids = lax.broadcasted_iota(jnp.int32, (1, clip_count), 1)
    level_ids = lax.broadcasted_iota(jnp.int32, (1, level_count), 1)
    tok_hot = clip_of[:, None] == clip_ids
    level_rows = jnp.sum(jnp.where(tok_hot, clip_level[None, :], 0), axis=1)
    level_hot = (level_rows[:, None] == level_ids).astype(jnp.float32)
    modulation = jnp.dot(level_hot, mod_table, precision=lax.Precision.HIGHEST)
    moduled = (activations.astype(jnp.float32) * (1.0 + modulation)).astype(jnp.bfloat16)
    qkv = jnp.einsum(
        "td,dchk->hctk", moduled, qkv_weight, preferred_element_type=jnp.float32
    ).astype(jnp.bfloat16)
    lane = head_size
    clip_rows = tok // lane
    pad_rows = -clip_rows % 8
    clip_slab = jnp.concatenate(
        [clip_of.astype(jnp.bfloat16).reshape(clip_rows, lane), jnp.zeros((pad_rows, lane), jnp.bfloat16)]
    )
    payload = jnp.concatenate(
        [qkv.reshape(heads_here, 3 * tok, lane), jnp.broadcast_to(clip_slab, (heads_here,) + clip_slab.shape)],
        axis=1,
    )
    exch = lax.all_to_all(payload, "yc", 0, 0, tiled=True)
    group_tok = heads_here * tok
    queries = exch[:, 0:tok].reshape(group_tok, lane)
    keys = exch[:, tok:2 * tok].reshape(group_tok, lane)
    values = exch[:, 2 * tok:3 * tok].reshape(group_tok, lane)
    clip_group = exch[:, 3 * tok:3 * tok + clip_rows].reshape(group_tok)
    group_rows = group_tok // lane
    kv_pad = -group_rows % 8
    kv_payload = jnp.concatenate(
        [keys, values, clip_group.reshape(group_rows, lane), jnp.zeros((kv_pad, lane), jnp.bfloat16)]
    )
    kv_all = lax.all_gather(kv_payload, "x", axis=0)
    key_clips = kv_all[:, 2 * group_tok:2 * group_tok + group_rows].reshape(kv_all.shape[0], group_tok)
    key_hot = (key_clips.astype(jnp.int32)[:, None, :] == clip_ids[0][None, :, None]).astype(jnp.bfloat16)
    query_hot = (clip_group.astype(jnp.int32)[:, None] == clip_ids).astype(jnp.float32)
    qvis = jnp.dot(query_hot, visible.astype(jnp.float32), precision=lax.Precision.HIGHEST).astype(jnp.bfloat16)
    score_scale = float(np.float32(1.0) / np.sqrt(np.float32(head_size)))
    attended = flash_attention1(
        qvis, queries, kv_all, key_hot, clip_group.astype(jnp.int32), key_clips.astype(jnp.int32), score_scale, group_tok
    )
    back = lax.all_to_all(attended.reshape(heads_here, tok, lane), "yc", 0, 0, tiled=True)
    mixed = jnp.einsum(
        "hrd,hdo->ro", back, out_weight, preferred_element_type=jnp.float32
    ).astype(jnp.bfloat16)
    groups = lax.axis_size("head")
    parts = mixed.reshape(groups, mixed.shape[0] // groups, mixed.shape[1])
    parts = lax.all_to_all(parts, "head", 0, 0)
    return jnp.sum(parts.astype(jnp.float32), axis=0).astype(jnp.bfloat16)


def solution(mesh):
    ctx = mesh.shape["ctx"]
    heads = 4
    fine = Mesh(mesh.devices.reshape(ctx // heads, heads, mesh.shape["head"]), ("x", "yc", "head"))
    placed = (
        P(("x", "yc"), None),
        P(None, None, "head", None),
        P("head", None, None),
        P(),
        P(),
        P(("x", "yc")),
        P(),
    )
    return jax.shard_map(
        per_device, mesh=fine, in_specs=placed, out_specs=P(("x", "yc", "head"), None), check_vma=False
    )
```

```python
import functools
import math

import jax
import numpy as np
import jax.numpy as jnp
from jax import lax
from jax.experimental import pallas as pl
from jax.experimental.pallas import tpu as pltpu
from jax.sharding import Mesh, PartitionSpec as P


def attn_kernel(qvis_ref, q_ref, kv_ref, kh_ref, o_ref, m_sc, l_sc, acc_sc, *, scale, nsteps, heads):
    j = pl.program_id(0)
    lanes = m_sc.shape[2]

    @pl.when(j == 0)
    def _():
        m_sc[...] = jnp.full(m_sc.shape, -1e30, jnp.float32)
        l_sc[...] = jnp.zeros(l_sc.shape, jnp.float32)
        acc_sc[...] = jnp.zeros(acc_sc.shape, jnp.float32)

    allowed = jnp.dot(qvis_ref[...], kh_ref[...], preferred_element_type=jnp.float32)
    bias = jnp.where(allowed > 0.5, 0.0, -jnp.inf).astype(jnp.float32)
    bk = bias.shape[1]
    for h in range(heads):
        s = lax.dot_general(q_ref[h], kv_ref[0, h], (((1,), (1,)), ((), ())), preferred_element_type=jnp.float32)
        s = s * scale + bias
        m_old = m_sc[h]
        m_new = jnp.maximum(m_old, jnp.max(s, axis=1, keepdims=True))
        p = jnp.exp(s - jnp.tile(m_new, (1, bk // lanes)))
        alpha = jnp.exp(m_old - m_new)
        l_sc[h] = l_sc[h] * alpha + jnp.sum(p, axis=1, keepdims=True)
        acc_sc[h] = acc_sc[h] * alpha + jnp.dot(
            p.astype(jnp.bfloat16), kv_ref[1, h], preferred_element_type=jnp.float32
        )
        m_sc[h] = m_new

    @pl.when(j == nsteps - 1)
    def _():
        hd = acc_sc.shape[2]
        for h in range(heads):
            o_ref[:, h * hd:(h + 1) * hd] = (acc_sc[h] / l_sc[h]).astype(o_ref.dtype)


def flash_attention(qvis, q, kv_all, key_hot, scale):
    heads, nq, hd = q.shape
    sources, _, _, tok, _ = kv_all.shape
    clip_count = qvis.shape[1]
    bk = math.gcd(tok, 512)
    sub = tok // bk
    nsteps = sources * sub
    kernel = functools.partial(attn_kernel, scale=scale, nsteps=nsteps, heads=heads)
    flops = 4 * heads * nq * sources * tok * hd + 2 * nq * clip_count * sources * tok
    cost = pl.CostEstimate(
        flops=flops,
        transcendentals=heads * nq * sources * tok,
        bytes_accessed=kv_all.size * 2 + q.size * 2 + nq * heads * hd * 2,
    )
    return pl.pallas_call(
        kernel,
        grid=(nsteps,),
        in_specs=[
            pl.BlockSpec((nq, clip_count), lambda j: (0, 0)),
            pl.BlockSpec((heads, nq, hd), lambda j: (0, 0, 0)),
            pl.BlockSpec((None, 2, heads, bk, hd), lambda j: (j // sub, 0, 0, j % sub, 0)),
            pl.BlockSpec((None, clip_count, bk), lambda j: (j // sub, 0, j % sub)),
        ],
        out_specs=pl.BlockSpec((nq, heads * hd), lambda j: (0, 0)),
        out_shape=jax.ShapeDtypeStruct((nq, heads * hd), jnp.bfloat16),
        scratch_shapes=[
            pltpu.VMEM((heads, nq, 128), jnp.float32),
            pltpu.VMEM((heads, nq, 128), jnp.float32),
            pltpu.VMEM((heads, nq, hd), jnp.float32),
        ],
        compiler_params=pltpu.CompilerParams(dimension_semantics=("arbitrary",)),
        cost_estimate=cost,
    )(qvis, q, kv_all, key_hot)


def attn_body(qvis_ref, q_ref, k_ref, v_ref, kh_ref, m_sc, l_sc, acc_sc, scale):
    lanes = m_sc.shape[1]
    allowed = jnp.dot(qvis_ref[...], kh_ref[...], preferred_element_type=jnp.float32)
    bias = jnp.where(allowed > 0.5, 0.0, -jnp.inf).astype(jnp.float32)
    bk = bias.shape[1]
    s = lax.dot_general(q_ref[...], k_ref[...], (((1,), (1,)), ((), ())), preferred_element_type=jnp.float32)
    s = s * scale + bias
    m_old = m_sc[...]
    m_new = jnp.maximum(m_old, jnp.max(s, axis=1, keepdims=True))
    p = jnp.exp(s - jnp.tile(m_new, (1, bk // lanes)))
    alpha = jnp.exp(m_old - m_new)
    l_sc[...] = l_sc[...] * alpha + jnp.sum(p, axis=1, keepdims=True)
    acc_sc[...] = acc_sc[...] * alpha + jnp.dot(
        p.astype(jnp.bfloat16), v_ref[...], preferred_element_type=jnp.float32
    )
    m_sc[...] = m_new


def local_kernel(qvis_ref, q_ref, k_ref, v_ref, kh_ref, m_ref, l_ref, acc_ref, *, scale):
    j = pl.program_id(0)

    @pl.when(j == 0)
    def _():
        m_ref[...] = jnp.full(m_ref.shape, -1e30, jnp.float32)
        l_ref[...] = jnp.zeros(l_ref.shape, jnp.float32)
        acc_ref[...] = jnp.zeros(acc_ref.shape, jnp.float32)

    attn_body(qvis_ref, q_ref, k_ref, v_ref, kh_ref, m_ref, l_ref, acc_ref, scale)


def remote_kernel(own_ref, qvis_ref, q_ref, k_ref, v_ref, kh_ref, m_in, l_in, acc_in, o_ref, m_sc, l_sc, acc_sc, *, scale, nsteps):
    j = pl.program_id(0)

    @pl.when(j == 0)
    def _():
        m_sc[...] = m_in[...]
        l_sc[...] = l_in[...]
        acc_sc[...] = acc_in[...]

    attn_body(qvis_ref, q_ref, k_ref, v_ref, kh_ref, m_sc, l_sc, acc_sc, scale)

    @pl.when(j == nsteps - 1)
    def _():
        o_ref[...] = (acc_sc[...] / l_sc[...]).astype(o_ref.dtype)


def attend_local(qvis, q, keys, values, key_hot, scale):
    nq, hd = q.shape
    tok = keys.shape[0]
    clip_count = qvis.shape[1]
    bk = math.gcd(tok, 512)
    nsteps = tok // bk
    state = jax.ShapeDtypeStruct((nq, 128), jnp.float32)
    return pl.pallas_call(
        functools.partial(local_kernel, scale=scale),
        grid=(nsteps,),
        in_specs=[
            pl.BlockSpec((nq, clip_count), lambda j: (0, 0)),
            pl.BlockSpec((nq, hd), lambda j: (0, 0)),
            pl.BlockSpec((bk, hd), lambda j: (j, 0)),
            pl.BlockSpec((bk, hd), lambda j: (j, 0)),
            pl.BlockSpec((clip_count, bk), lambda j: (0, j)),
        ],
        out_specs=[
            pl.BlockSpec((nq, 128), lambda j: (0, 0)),
            pl.BlockSpec((nq, 128), lambda j: (0, 0)),
            pl.BlockSpec((nq, hd), lambda j: (0, 0)),
        ],
        out_shape=[state, state, jax.ShapeDtypeStruct((nq, hd), jnp.float32)],
        compiler_params=pltpu.CompilerParams(dimension_semantics=("arbitrary",)),
        cost_estimate=pl.CostEstimate(
            flops=4 * nq * tok * hd + 2 * nq * clip_count * tok,
            transcendentals=nq * tok,
            bytes_accessed=4 * tok * hd + 3 * nq * 512,
        ),
    )(qvis, q, keys, values, key_hot)


def attend_remote(own, qvis, q, kv_all, key_hot, carry, scale, tok):
    nq, hd = q.shape
    sources = kv_all.shape[0]
    clip_count = qvis.shape[1]
    bk = math.gcd(tok, 512)
    sub = tok // bk
    nsteps = (sources - 1) * sub

    def src(j, o):
        return (o[0] + 1 + j // sub) % sources

    kernel = functools.partial(remote_kernel, scale=scale, nsteps=nsteps)
    grid_spec = pltpu.PrefetchScalarGridSpec(
        num_scalar_prefetch=1,
        grid=(nsteps,),
        in_specs=[
            pl.BlockSpec((nq, clip_count), lambda j, o: (0, 0)),
            pl.BlockSpec((nq, hd), lambda j, o: (0, 0)),
            pl.BlockSpec((None, bk, hd), lambda j, o: (src(j, o), j % sub, 0)),
            pl.BlockSpec((None, bk, hd), lambda j, o: (src(j, o), sub + j % sub, 0)),
            pl.BlockSpec((None, clip_count, bk), lambda j, o: (src(j, o), 0, j % sub)),
            pl.BlockSpec((nq, 128), lambda j, o: (0, 0)),
            pl.BlockSpec((nq, 128), lambda j, o: (0, 0)),
            pl.BlockSpec((nq, hd), lambda j, o: (0, 0)),
        ],
        out_specs=pl.BlockSpec((nq, hd), lambda j, o: (0, 0)),
        scratch_shapes=[
            pltpu.VMEM((nq, 128), jnp.float32),
            pltpu.VMEM((nq, 128), jnp.float32),
            pltpu.VMEM((nq, hd), jnp.float32),
        ],
    )
    return pl.pallas_call(
        kernel,
        grid_spec=grid_spec,
        out_shape=jax.ShapeDtypeStruct((nq, hd), jnp.bfloat16),
        compiler_params=pltpu.CompilerParams(dimension_semantics=("arbitrary",)),
        cost_estimate=pl.CostEstimate(
            flops=4 * nq * (sources - 1) * tok * hd + 2 * nq * clip_count * (sources - 1) * tok,
            transcendentals=nq * (sources - 1) * tok,
            bytes_accessed=kv_all.size * 2 + 3 * nq * 512,
        ),
    )(own, qvis, q, kv_all, kv_all, key_hot, *carry)


def per_device(activations, qkv_weight, out_weight, mod_table, clip_level, clip_of, visible):
    heads_here = qkv_weight.shape[2]
    head_size = qkv_weight.shape[3]
    clip_count = visible.shape[0]
    level_count = mod_table.shape[0]
    tok = clip_of.shape[0]
    clip_ids = lax.broadcasted_iota(jnp.int32, (1, clip_count), 1)
    level_ids = lax.broadcasted_iota(jnp.int32, (1, level_count), 1)
    tok_hot = clip_of[:, None] == clip_ids
    level_rows = jnp.sum(jnp.where(tok_hot, clip_level[None, :], 0), axis=1)
    level_hot = (level_rows[:, None] == level_ids).astype(jnp.float32)
    modulation = jnp.dot(level_hot, mod_table, precision=lax.Precision.HIGHEST)
    moduled = (activations.astype(jnp.float32) * (1.0 + modulation)).astype(jnp.bfloat16)
    qkv = jnp.einsum(
        "td,dchk->hctk", moduled, qkv_weight, preferred_element_type=jnp.float32
    ).astype(jnp.bfloat16)
    lane = head_size
    clip_rows = tok // lane
    pad_rows = -clip_rows % 8
    clip_slab = jnp.concatenate(
        [clip_of.astype(jnp.bfloat16).reshape(clip_rows, lane), jnp.zeros((pad_rows, lane), jnp.bfloat16)]
    )
    payload = jnp.concatenate(
        [qkv.reshape(heads_here, 3 * tok, lane), jnp.broadcast_to(clip_slab, (heads_here,) + clip_slab.shape)],
        axis=1,
    )
    exch = lax.all_to_all(payload, "yc", 0, 0, tiled=True)
    group_tok = heads_here * tok
    queries = exch[:, 0:tok].reshape(group_tok, lane)
    keys = exch[:, tok:2 * tok].reshape(group_tok, lane)
    values = exch[:, 2 * tok:3 * tok].reshape(group_tok, lane)
    clip_group = exch[:, 3 * tok:3 * tok + clip_rows].reshape(group_tok)
    group_rows = group_tok // lane
    kv_pad = -group_rows % 8
    kv_payload = jnp.concatenate(
        [keys, values, clip_group.reshape(group_rows, lane), jnp.zeros((kv_pad, lane), jnp.bfloat16)]
    )
    query_hot = (clip_group.astype(jnp.int32)[:, None] == clip_ids).astype(jnp.float32)
    qvis = jnp.dot(query_hot, visible.astype(jnp.float32), precision=lax.Precision.HIGHEST).astype(jnp.bfloat16)
    score_scale = float(np.float32(1.0) / np.sqrt(np.float32(head_size)))
    local_hot = (clip_group.astype(jnp.int32)[None, :] == clip_ids[0][:, None]).astype(jnp.bfloat16)
    carry = attend_local(qvis, queries, keys, values, local_hot, score_scale)
    kv_all = lax.all_gather(kv_payload, "x", axis=0)
    key_clips = kv_all[:, 2 * group_tok:2 * group_tok + group_rows].reshape(kv_all.shape[0], group_tok)
    key_hot = (key_clips.astype(jnp.int32)[:, None, :] == clip_ids[0][None, :, None]).astype(jnp.bfloat16)
    own = lax.axis_index("x").reshape(1).astype(jnp.int32)
    attended = attend_remote(own, qvis, queries, kv_all, key_hot, carry, score_scale, group_tok)
    back = lax.all_to_all(attended.reshape(heads_here, tok, lane), "yc", 0, 0, tiled=True)
    mixed = jnp.einsum(
        "hrd,hdo->ro", back, out_weight, preferred_element_type=jnp.float32
    ).astype(jnp.bfloat16)
    groups = lax.axis_size("head")
    parts = mixed.reshape(groups, mixed.shape[0] // groups, mixed.shape[1])
    parts = lax.all_to_all(parts, "head", 0, 0)
    return jnp.sum(parts.astype(jnp.float32), axis=0).astype(jnp.bfloat16)


def solution(mesh):
    ctx = mesh.shape["ctx"]
    heads = 4
    fine = Mesh(mesh.devices.reshape(ctx // heads, heads, mesh.shape["head"]), ("x", "yc", "head"))
    placed = (
        P(("x", "yc"), None),
        P(None, None, "head", None),
        P("head", None, None),
        P(),
        P(),
        P(("x", "yc")),
        P(),
    )
    return jax.shard_map(
        per_device, mesh=fine, in_specs=placed, out_specs=P(("x", "yc", "head"), None), check_vma=False
    )
```

```python
import functools
import math

import jax
import numpy as np
import jax.numpy as jnp
from jax import lax
from jax.experimental import pallas as pl
from jax.experimental.pallas import tpu as pltpu
from jax.sharding import Mesh, PartitionSpec as P


def attn_kernel(qvis_ref, q_ref, kv_ref, kh_ref, o_ref, m_sc, l_sc, acc_sc, *, scale, nsteps, heads):
    j = pl.program_id(0)
    lanes = m_sc.shape[2]

    @pl.when(j == 0)
    def _():
        m_sc[...] = jnp.full(m_sc.shape, -1e30, jnp.float32)
        l_sc[...] = jnp.zeros(l_sc.shape, jnp.float32)
        acc_sc[...] = jnp.zeros(acc_sc.shape, jnp.float32)

    allowed = jnp.dot(qvis_ref[...], kh_ref[...], preferred_element_type=jnp.float32)
    bias = jnp.where(allowed > 0.5, 0.0, -jnp.inf).astype(jnp.float32)
    bk = bias.shape[1]
    for h in range(heads):
        s = lax.dot_general(q_ref[h], kv_ref[0, h], (((1,), (1,)), ((), ())), preferred_element_type=jnp.float32)
        s = s * scale + bias
        m_old = m_sc[h]
        m_new = jnp.maximum(m_old, jnp.max(s, axis=1, keepdims=True))
        p = jnp.exp(s - jnp.tile(m_new, (1, bk // lanes)))
        alpha = jnp.exp(m_old - m_new)
        l_sc[h] = l_sc[h] * alpha + jnp.sum(p, axis=1, keepdims=True)
        acc_sc[h] = acc_sc[h] * alpha + jnp.dot(
            p.astype(jnp.bfloat16), kv_ref[1, h], preferred_element_type=jnp.float32
        )
        m_sc[h] = m_new

    @pl.when(j == nsteps - 1)
    def _():
        hd = acc_sc.shape[2]
        for h in range(heads):
            o_ref[:, h * hd:(h + 1) * hd] = (acc_sc[h] / l_sc[h]).astype(o_ref.dtype)


def flash_attention(qvis, q, kv_all, key_hot, scale):
    heads, nq, hd = q.shape
    sources, _, _, tok, _ = kv_all.shape
    clip_count = qvis.shape[1]
    bk = math.gcd(tok, 512)
    sub = tok // bk
    nsteps = sources * sub
    kernel = functools.partial(attn_kernel, scale=scale, nsteps=nsteps, heads=heads)
    flops = 4 * heads * nq * sources * tok * hd + 2 * nq * clip_count * sources * tok
    cost = pl.CostEstimate(
        flops=flops,
        transcendentals=heads * nq * sources * tok,
        bytes_accessed=kv_all.size * 2 + q.size * 2 + nq * heads * hd * 2,
    )
    return pl.pallas_call(
        kernel,
        grid=(nsteps,),
        in_specs=[
            pl.BlockSpec((nq, clip_count), lambda j: (0, 0)),
            pl.BlockSpec((heads, nq, hd), lambda j: (0, 0, 0)),
            pl.BlockSpec((None, 2, heads, bk, hd), lambda j: (j // sub, 0, 0, j % sub, 0)),
            pl.BlockSpec((None, clip_count, bk), lambda j: (j // sub, 0, j % sub)),
        ],
        out_specs=pl.BlockSpec((nq, heads * hd), lambda j: (0, 0)),
        out_shape=jax.ShapeDtypeStruct((nq, heads * hd), jnp.bfloat16),
        scratch_shapes=[
            pltpu.VMEM((heads, nq, 128), jnp.float32),
            pltpu.VMEM((heads, nq, 128), jnp.float32),
            pltpu.VMEM((heads, nq, hd), jnp.float32),
        ],
        compiler_params=pltpu.CompilerParams(dimension_semantics=("arbitrary",)),
        cost_estimate=cost,
    )(qvis, q, kv_all, key_hot)


def attn_body(qvis_ref, q_ref, k_ref, v_ref, kh_ref, m_sc, l_sc, acc_sc, scale):
    lanes = m_sc.shape[1]
    allowed = jnp.dot(qvis_ref[...], kh_ref[...], preferred_element_type=jnp.float32)
    bias = jnp.where(allowed > 0.5, 0.0, -jnp.inf).astype(jnp.float32)
    bk = bias.shape[1]
    s = lax.dot_general(q_ref[...], k_ref[...], (((1,), (1,)), ((), ())), preferred_element_type=jnp.float32)
    s = s * scale + bias
    m_old = m_sc[...]
    m_new = jnp.maximum(m_old, jnp.max(s, axis=1, keepdims=True))
    p = jnp.exp(s - jnp.tile(m_new, (1, bk // lanes)))
    alpha = jnp.exp(m_old - m_new)
    l_sc[...] = l_sc[...] * alpha + jnp.sum(p, axis=1, keepdims=True)
    acc_sc[...] = acc_sc[...] * alpha + jnp.dot(
        p.astype(jnp.bfloat16), v_ref[...], preferred_element_type=jnp.float32
    )
    m_sc[...] = m_new


def local_kernel(qvis_ref, q_ref, k_ref, v_ref, kh_ref, m_ref, l_ref, acc_ref, *, scale):
    j = pl.program_id(0)

    @pl.when(j == 0)
    def _():
        m_ref[...] = jnp.full(m_ref.shape, -1e30, jnp.float32)
        l_ref[...] = jnp.zeros(l_ref.shape, jnp.float32)
        acc_ref[...] = jnp.zeros(acc_ref.shape, jnp.float32)

    attn_body(qvis_ref, q_ref, k_ref, v_ref, kh_ref, m_ref, l_ref, acc_ref, scale)


def remote_kernel(own_ref, qvis_ref, q_ref, k_ref, v_ref, kh_ref, m_in, l_in, acc_in, o_ref, m_sc, l_sc, acc_sc, *, scale, nsteps):
    j = pl.program_id(0)

    @pl.when(j == 0)
    def _():
        m_sc[...] = m_in[...]
        l_sc[...] = l_in[...]
        acc_sc[...] = acc_in[...]

    attn_body(qvis_ref, q_ref, k_ref, v_ref, kh_ref, m_sc, l_sc, acc_sc, scale)

    @pl.when(j == nsteps - 1)
    def _():
        o_ref[...] = (acc_sc[...] / l_sc[...]).astype(o_ref.dtype)


def attend_local(qvis, q, keys, values, key_hot, scale):
    nq, hd = q.shape
    tok = keys.shape[0]
    clip_count = qvis.shape[1]
    bk = math.gcd(tok, 512)
    nsteps = tok // bk
    state = jax.ShapeDtypeStruct((nq, 128), jnp.float32)
    return pl.pallas_call(
        functools.partial(local_kernel, scale=scale),
        grid=(nsteps,),
        in_specs=[
            pl.BlockSpec((nq, clip_count), lambda j: (0, 0)),
            pl.BlockSpec((nq, hd), lambda j: (0, 0)),
            pl.BlockSpec((bk, hd), lambda j: (j, 0)),
            pl.BlockSpec((bk, hd), lambda j: (j, 0)),
            pl.BlockSpec((clip_count, bk), lambda j: (0, j)),
        ],
        out_specs=[
            pl.BlockSpec((nq, 128), lambda j: (0, 0)),
            pl.BlockSpec((nq, 128), lambda j: (0, 0)),
            pl.BlockSpec((nq, hd), lambda j: (0, 0)),
        ],
        out_shape=[state, state, jax.ShapeDtypeStruct((nq, hd), jnp.float32)],
        compiler_params=pltpu.CompilerParams(dimension_semantics=("arbitrary",)),
        cost_estimate=pl.CostEstimate(
            flops=4 * nq * tok * hd + 2 * nq * clip_count * tok,
            transcendentals=nq * tok,
            bytes_accessed=4 * tok * hd + 3 * nq * 512,
        ),
    )(qvis, q, keys, values, key_hot)


def attend_remote(own, qvis, q, kv_all, key_hot, carry, scale, tok, part, parts):
    nq, hd = q.shape
    nq = nq // parts
    sources = kv_all.shape[0]
    clip_count = qvis.shape[1]
    bk = math.gcd(tok, 512)
    sub = tok // bk
    nsteps = (sources - 1) * sub

    def src(j, o):
        return (o[0] + 1 + j // sub) % sources

    kernel = functools.partial(remote_kernel, scale=scale, nsteps=nsteps)
    grid_spec = pltpu.PrefetchScalarGridSpec(
        num_scalar_prefetch=1,
        grid=(nsteps,),
        in_specs=[
            pl.BlockSpec((nq, clip_count), lambda j, o: (part, 0)),
            pl.BlockSpec((nq, hd), lambda j, o: (part, 0)),
            pl.BlockSpec((None, bk, hd), lambda j, o: (src(j, o), j % sub, 0)),
            pl.BlockSpec((None, bk, hd), lambda j, o: (src(j, o), sub + j % sub, 0)),
            pl.BlockSpec((None, clip_count, bk), lambda j, o: (src(j, o), 0, j % sub)),
            pl.BlockSpec((nq, 128), lambda j, o: (part, 0)),
            pl.BlockSpec((nq, 128), lambda j, o: (part, 0)),
            pl.BlockSpec((nq, hd), lambda j, o: (part, 0)),
        ],
        out_specs=pl.BlockSpec((nq, hd), lambda j, o: (0, 0)),
        scratch_shapes=[
            pltpu.VMEM((nq, 128), jnp.float32),
            pltpu.VMEM((nq, 128), jnp.float32),
            pltpu.VMEM((nq, hd), jnp.float32),
        ],
    )
    return pl.pallas_call(
        kernel,
        grid_spec=grid_spec,
        out_shape=jax.ShapeDtypeStruct((nq, hd), jnp.bfloat16),
        compiler_params=pltpu.CompilerParams(dimension_semantics=("arbitrary",)),
        cost_estimate=pl.CostEstimate(
            flops=4 * nq * (sources - 1) * tok * hd + 2 * nq * clip_count * (sources - 1) * tok,
            transcendentals=nq * (sources - 1) * tok,
            bytes_accessed=kv_all.size * 2 + 3 * nq * 512,
        ),
    )(own, qvis, q, kv_all, kv_all, key_hot, *carry)


def per_device(activations, qkv_weight, out_weight, mod_table, clip_level, clip_of, visible):
    heads_here = qkv_weight.shape[2]
    head_size = qkv_weight.shape[3]
    clip_count = visible.shape[0]
    level_count = mod_table.shape[0]
    tok = clip_of.shape[0]
    clip_ids = lax.broadcasted_iota(jnp.int32, (1, clip_count), 1)
    level_rows = jnp.take(clip_level, clip_of, axis=0)
    modulation = jnp.take(mod_table, level_rows, axis=0)
    moduled = (activations.astype(jnp.float32) * (1.0 + modulation)).astype(jnp.bfloat16)
    qkv = jnp.einsum(
        "td,dchk->hctk", moduled, qkv_weight, preferred_element_type=jnp.float32
    ).astype(jnp.bfloat16)
    lane = head_size
    clip_rows = tok // lane
    pad_rows = -clip_rows % 8
    clip_slab = jnp.concatenate(
        [clip_of.astype(jnp.bfloat16).reshape(clip_rows, lane), jnp.zeros((pad_rows, lane), jnp.bfloat16)]
    )
    payload = jnp.concatenate(
        [qkv.reshape(heads_here, 3 * tok, lane), jnp.broadcast_to(clip_slab, (heads_here,) + clip_slab.shape)],
        axis=1,
    )
    exch = lax.all_to_all(payload, "yc", 0, 0, tiled=True)
    group_tok = heads_here * tok
    queries = exch[:, 0:tok].reshape(group_tok, lane)
    keys = exch[:, tok:2 * tok].reshape(group_tok, lane)
    values = exch[:, 2 * tok:3 * tok].reshape(group_tok, lane)
    clip_group = exch[:, 3 * tok:3 * tok + clip_rows].reshape(group_tok)
    group_rows = group_tok // lane
    kv_pad = -group_rows % 8
    kv_payload = jnp.concatenate(
        [keys, values, clip_group.reshape(group_rows, lane), jnp.zeros((kv_pad, lane), jnp.bfloat16)]
    )
    blocks = lax.axis_size("head")
    parts = 2
    piece = tok // (parts * blocks)

    def split_rows(a):
        rest = a.shape[1:]
        a = a.reshape((heads_here, blocks, parts, piece) + rest)
        return jnp.moveaxis(a, 2, 0).reshape((group_tok,) + rest)

    q_ord = split_rows(queries)
    clip_q = split_rows(clip_group).astype(jnp.int32)
    query_hot = (clip_q[:, None] == clip_ids).astype(jnp.float32)
    qvis = jnp.dot(query_hot, visible.astype(jnp.float32), precision=lax.Precision.HIGHEST).astype(jnp.bfloat16)
    score_scale = float(np.float32(1.0) / np.sqrt(np.float32(head_size)))
    local_hot = (clip_group.astype(jnp.int32)[None, :] == clip_ids[0][:, None]).astype(jnp.bfloat16)
    carry = attend_local(qvis, q_ord, keys, values, local_hot, score_scale)
    kv_all = lax.all_gather(kv_payload, "x", axis=0)
    key_clips = kv_all[:, 2 * group_tok:2 * group_tok + group_rows].reshape(kv_all.shape[0], group_tok)
    key_hot = (key_clips.astype(jnp.int32)[:, None, :] == clip_ids[0][None, :, None]).astype(jnp.bfloat16)
    own = lax.axis_index("x").reshape(1).astype(jnp.int32)
    outs = []
    for part in range(parts):
        attended = attend_remote(own, qvis, q_ord, kv_all, key_hot, carry, score_scale, group_tok, part, parts)
        back = lax.all_to_all(attended.reshape(heads_here, blocks * piece, lane), "yc", 0, 0, tiled=True)
        mixed = jnp.einsum(
            "hrd,hdo->ro", back, out_weight, preferred_element_type=jnp.float32
        ).astype(jnp.bfloat16)
        if part == 0:
            outs.append(lax.psum_scatter(mixed, "head", scatter_dimension=0, tiled=True))
        else:
            pieces = lax.all_to_all(mixed.reshape(blocks, piece, mixed.shape[1]), "head", 0, 0)
            outs.append(jnp.sum(pieces.astype(jnp.float32), axis=0).astype(jnp.bfloat16))
    return jnp.concatenate(outs, axis=0)


def solution(mesh):
    ctx = mesh.shape["ctx"]
    heads = 4
    fine = Mesh(mesh.devices.reshape(ctx // heads, heads, mesh.shape["head"]), ("x", "yc", "head"))
    placed = (
        P(("x", "yc"), None),
        P(None, None, "head", None),
        P("head", None, None),
        P(),
        P(),
        P(("x", "yc")),
        P(),
    )
    return jax.shard_map(
        per_device, mesh=fine, in_specs=placed, out_specs=P(("x", "yc", "head"), None), check_vma=False
    )
```

```python
import functools
import math

import jax
import numpy as np
import jax.numpy as jnp
from jax import lax
from jax.experimental import pallas as pl
from jax.experimental.pallas import tpu as pltpu
from jax.sharding import Mesh, PartitionSpec as P


def attn_body(qvis_ref, q_ref, k_ref, v_ref, kh_ref, m_sc, l_sc, acc_sc, scale):
    lanes = m_sc.shape[1]
    allowed = jnp.dot(qvis_ref[...], kh_ref[...], preferred_element_type=jnp.float32)
    s = lax.dot_general(q_ref[...], k_ref[...], (((1,), (1,)), ((), ())), preferred_element_type=jnp.float32)
    bk = s.shape[1]
    s = jnp.where(allowed > 0.5, s * scale, -jnp.inf)
    m_old = m_sc[...]
    m_new = jnp.maximum(m_old, jnp.max(s, axis=1, keepdims=True))
    p = jnp.exp2(s - jnp.tile(m_new, (1, bk // lanes)))
    alpha = jnp.exp2(m_old - m_new)
    l_sc[...] = l_sc[...] * alpha + jnp.sum(p, axis=1, keepdims=True)
    acc_sc[...] = acc_sc[...] * alpha + jnp.dot(
        p.astype(jnp.bfloat16), v_ref[...], preferred_element_type=jnp.float32
    )
    m_sc[...] = m_new


def local_kernel(qvis_ref, q_ref, k_ref, v_ref, kh_ref, m_ref, l_ref, acc_ref, *, scale):
    j = pl.program_id(0)

    @pl.when(j == 0)
    def _():
        m_ref[...] = jnp.full(m_ref.shape, -1e30, jnp.float32)
        l_ref[...] = jnp.zeros(l_ref.shape, jnp.float32)
        acc_ref[...] = jnp.zeros(acc_ref.shape, jnp.float32)

    attn_body(qvis_ref, q_ref, k_ref, v_ref, kh_ref, m_ref, l_ref, acc_ref, scale)


def remote_kernel(own_ref, qvis_ref, q_ref, k_ref, v_ref, kh_ref, m_in, l_in, acc_in, o_ref, m_sc, l_sc, acc_sc, *, scale, nsteps):
    j = pl.program_id(0)

    @pl.when(j == 0)
    def _():
        m_sc[...] = m_in[...]
        l_sc[...] = l_in[...]
        acc_sc[...] = acc_in[...]

    attn_body(qvis_ref, q_ref, k_ref, v_ref, kh_ref, m_sc, l_sc, acc_sc, scale)

    @pl.when(j == nsteps - 1)
    def _():
        o_ref[...] = (acc_sc[...] / l_sc[...]).astype(o_ref.dtype)


def carry_kernel(own_ref, qvis_ref, q_ref, k_ref, v_ref, kh_ref, m_in, l_in, acc_in, m_ref, l_ref, acc_ref, *, scale):
    j = pl.program_id(0)

    @pl.when(j == 0)
    def _():
        m_ref[...] = m_in[...]
        l_ref[...] = l_in[...]
        acc_ref[...] = acc_in[...]

    attn_body(qvis_ref, q_ref, k_ref, v_ref, kh_ref, m_ref, l_ref, acc_ref, scale)


def attend_local(qvis, q, keys, values, key_hot, scale):
    nq, hd = q.shape
    tok = keys.shape[0]
    clip_count = qvis.shape[1]
    bk = math.gcd(tok, 1024)
    nsteps = tok // bk
    state = jax.ShapeDtypeStruct((nq, 128), jnp.float32)
    return pl.pallas_call(
        functools.partial(local_kernel, scale=scale),
        grid=(nsteps,),
        in_specs=[
            pl.BlockSpec((nq, clip_count), lambda j: (0, 0)),
            pl.BlockSpec((nq, hd), lambda j: (0, 0)),
            pl.BlockSpec((bk, hd), lambda j: (j, 0)),
            pl.BlockSpec((bk, hd), lambda j: (j, 0)),
            pl.BlockSpec((clip_count, bk), lambda j: (0, j)),
        ],
        out_specs=[
            pl.BlockSpec((nq, 128), lambda j: (0, 0)),
            pl.BlockSpec((nq, 128), lambda j: (0, 0)),
            pl.BlockSpec((nq, hd), lambda j: (0, 0)),
        ],
        out_shape=[state, state, jax.ShapeDtypeStruct((nq, hd), jnp.float32)],
        compiler_params=pltpu.CompilerParams(dimension_semantics=("arbitrary",)),
        cost_estimate=pl.CostEstimate(
            flops=4 * nq * tok * hd + 2 * nq * clip_count * tok,
            transcendentals=nq * tok,
            bytes_accessed=4 * tok * hd + 3 * nq * 512,
        ),
    )(qvis, q, keys, values, key_hot)


def attend_remote(own, qvis, q, kv_all, key_hot, carry, scale, tok, finalize):
    nq, hd = q.shape
    sources = kv_all.shape[0]
    clip_count = qvis.shape[1]
    bk = math.gcd(tok, 1024)
    sub = tok // bk
    nsteps = (sources - 1) * sub

    def src(j, o):
        return (o[0] + 1 + j // sub) % sources

    state_specs = [
        pl.BlockSpec((nq, 128), lambda j, o: (0, 0)),
        pl.BlockSpec((nq, 128), lambda j, o: (0, 0)),
        pl.BlockSpec((nq, hd), lambda j, o: (0, 0)),
    ]
    if finalize:
        kernel = functools.partial(remote_kernel, scale=scale, nsteps=nsteps)
        out_specs = pl.BlockSpec((nq, hd), lambda j, o: (0, 0))
        out_shape = jax.ShapeDtypeStruct((nq, hd), jnp.bfloat16)
        scratch = [
            pltpu.VMEM((nq, 128), jnp.float32),
            pltpu.VMEM((nq, 128), jnp.float32),
            pltpu.VMEM((nq, hd), jnp.float32),
        ]
    else:
        kernel = functools.partial(carry_kernel, scale=scale)
        out_specs = state_specs
        state = jax.ShapeDtypeStruct((nq, 128), jnp.float32)
        out_shape = [state, state, jax.ShapeDtypeStruct((nq, hd), jnp.float32)]
        scratch = []
    grid_spec = pltpu.PrefetchScalarGridSpec(
        num_scalar_prefetch=1,
        grid=(nsteps,),
        in_specs=[
            pl.BlockSpec((nq, clip_count), lambda j, o: (0, 0)),
            pl.BlockSpec((nq, hd), lambda j, o: (0, 0)),
            pl.BlockSpec((None, bk, hd), lambda j, o: (src(j, o), j % sub, 0)),
            pl.BlockSpec((None, bk, hd), lambda j, o: (src(j, o), sub + j % sub, 0)),
            pl.BlockSpec((None, clip_count, bk), lambda j, o: (src(j, o), 0, j % sub)),
        ] + state_specs,
        out_specs=out_specs,
        scratch_shapes=scratch,
    )
    return pl.pallas_call(
        kernel,
        grid_spec=grid_spec,
        out_shape=out_shape,
        compiler_params=pltpu.CompilerParams(dimension_semantics=("arbitrary",)),
        cost_estimate=pl.CostEstimate(
            flops=4 * nq * (sources - 1) * tok * hd + 2 * nq * clip_count * (sources - 1) * tok,
            transcendentals=nq * (sources - 1) * tok,
            bytes_accessed=kv_all.size * 2 + 3 * nq * 512,
        ),
    )(own, qvis, q, kv_all, kv_all, key_hot, *carry)


def per_device_body(activations, qkv_weight, out_weight, mod_table, clip_level, clip_of, visible):
    heads_here = qkv_weight.shape[2]
    head_size = qkv_weight.shape[3]
    clip_count = visible.shape[0]
    level_count = mod_table.shape[0]
    tok = clip_of.shape[0]
    clip_ids = lax.broadcasted_iota(jnp.int32, (1, clip_count), 1)
    level_ids = lax.broadcasted_iota(jnp.int32, (1, level_count), 1)
    tok_hot = clip_of[:, None] == clip_ids
    level_rows = jnp.sum(jnp.where(tok_hot, clip_level[None, :], 0), axis=1)
    level_hot = (level_rows[:, None] == level_ids).astype(jnp.float32)
    modulation = jnp.dot(level_hot, mod_table, precision=lax.Precision.HIGHEST)
    moduled = (activations.astype(jnp.float32) * (1.0 + modulation)).astype(jnp.bfloat16)
    qkv = jnp.einsum(
        "td,dchk->hctk", moduled, qkv_weight, preferred_element_type=jnp.float32
    ).astype(jnp.bfloat16)
    lane = head_size
    clip_rows = tok // lane
    pad_rows = -clip_rows % 8
    clip_slab = jnp.concatenate(
        [clip_of.astype(jnp.bfloat16).reshape(clip_rows, lane), jnp.zeros((pad_rows, lane), jnp.bfloat16)]
    )
    payload = jnp.concatenate(
        [qkv.reshape(heads_here, 3 * tok, lane), jnp.broadcast_to(clip_slab, (heads_here,) + clip_slab.shape)],
        axis=1,
    )
    exch = lax.all_to_all(payload, "yc", 0, 0, tiled=True)
    group_tok = heads_here * tok
    queries = exch[:, 0:tok].reshape(group_tok, lane)
    keys = exch[:, tok:2 * tok].reshape(group_tok, lane)
    values = exch[:, 2 * tok:3 * tok].reshape(group_tok, lane)
    clip_group = exch[:, 3 * tok:3 * tok + clip_rows].reshape(group_tok)
    halves = 2
    half_tok = group_tok // halves
    half_rows = half_tok // lane
    kv_pad = -half_rows % 8
    payloads = [
        jnp.concatenate(
            [
                keys[i * half_tok:(i + 1) * half_tok],
                values[i * half_tok:(i + 1) * half_tok],
                clip_group[i * half_tok:(i + 1) * half_tok].reshape(half_rows, lane),
                jnp.zeros((kv_pad, lane), jnp.bfloat16),
            ]
        )
        for i in range(halves)
    ]
    query_hot = (clip_group.astype(jnp.int32)[:, None] == clip_ids).astype(jnp.float32)
    qvis = jnp.dot(query_hot, visible.astype(jnp.float32), precision=lax.Precision.HIGHEST).astype(jnp.bfloat16)
    score_scale = float(np.float32(1.0) / np.sqrt(np.float32(head_size)) * np.float32(math.log2(math.e)))
    local_hot = (clip_group.astype(jnp.int32)[None, :] == clip_ids[0][:, None]).astype(jnp.bfloat16)
    carry = attend_local(qvis, queries, keys, values, local_hot, score_scale)
    own = lax.axis_index("x").reshape(1).astype(jnp.int32)
    gathered = []
    for i in range(halves):
        gathered.append(lax.all_gather(payloads[i], "x", axis=0))
    for i in range(halves):
        kv_all = gathered[i]
        key_clips = kv_all[:, 2 * half_tok:2 * half_tok + half_rows].reshape(kv_all.shape[0], half_tok)
        key_hot = (key_clips.astype(jnp.int32)[:, None, :] == clip_ids[0][None, :, None]).astype(jnp.bfloat16)
        carry = attend_remote(own, qvis, queries, kv_all, key_hot, carry, score_scale, half_tok, i == halves - 1)
    attended = carry
    back = lax.all_to_all(attended.reshape(heads_here, tok, lane), "yc", 0, 0, tiled=True)
    mixed = jnp.einsum(
        "hrd,hdo->ro", back, out_weight, preferred_element_type=jnp.float32
    ).astype(jnp.bfloat16)
    groups = lax.axis_size("head")
    parts = mixed.reshape(groups, mixed.shape[0] // groups, mixed.shape[1])
    parts = lax.all_to_all(parts, "head", 0, 0)
    return jnp.sum(parts.astype(jnp.float32), axis=0).astype(jnp.bfloat16)


def solution(mesh):
    ctx = mesh.shape["ctx"]
    heads = 4
    fine = Mesh(mesh.devices.reshape(ctx // heads, heads, mesh.shape["head"]), ("x", "yc", "head"))
    placed = (
        P(("x", "yc"), None),
        P(None, None, "head", None),
        P("head", None, None),
        P(),
        P(),
        P(("x", "yc")),
        P(),
    )
    return jax.shard_map(
        per_device_body, mesh=fine, in_specs=placed, out_specs=P(("x", "yc", "head"), None), check_vma=False
    )
```

```python
import functools
import math

import jax
import numpy as np
import jax.numpy as jnp
from jax import lax
from jax.experimental import pallas as pl
from jax.experimental.pallas import tpu as pltpu
from jax.sharding import Mesh, PartitionSpec as P


def attn_body(qvis_ref, q_ref, k_ref, v_ref, kh_ref, m_sc, l_sc, acc_sc, scale):
    lanes = m_sc.shape[1]
    allowed = jnp.dot(qvis_ref[...], kh_ref[...], preferred_element_type=jnp.float32)
    s = lax.dot_general(q_ref[...], k_ref[...], (((1,), (1,)), ((), ())), preferred_element_type=jnp.float32)
    bk = s.shape[1]
    s = jnp.where(allowed > 0.5, s * scale, -jnp.inf)
    m_old = m_sc[...]
    m_new = jnp.maximum(m_old, jnp.max(s, axis=1, keepdims=True))
    p = jnp.exp2(s - jnp.tile(m_new, (1, bk // lanes)))
    alpha = jnp.exp2(m_old - m_new)
    l_sc[...] = l_sc[...] * alpha + jnp.sum(p, axis=1, keepdims=True)
    acc_sc[...] = acc_sc[...] * alpha + jnp.dot(
        p.astype(jnp.bfloat16), v_ref[...], preferred_element_type=jnp.float32
    )
    m_sc[...] = m_new


def local_kernel(qvis_ref, q_ref, k_ref, v_ref, kh_ref, m_ref, l_ref, acc_ref, *, scale):
    j = pl.program_id(0)

    @pl.when(j == 0)
    def _():
        m_ref[...] = jnp.full(m_ref.shape, -1e30, jnp.float32)
        l_ref[...] = jnp.zeros(l_ref.shape, jnp.float32)
        acc_ref[...] = jnp.zeros(acc_ref.shape, jnp.float32)

    attn_body(qvis_ref, q_ref, k_ref, v_ref, kh_ref, m_ref, l_ref, acc_ref, scale)


def remote_kernel(own_ref, qvis_ref, q_ref, k_ref, v_ref, kh_ref, m_in, l_in, acc_in, o_ref, m_sc, l_sc, acc_sc, *, scale, nsteps):
    j = pl.program_id(0)

    @pl.when(j == 0)
    def _():
        m_sc[...] = m_in[...]
        l_sc[...] = l_in[...]
        acc_sc[...] = acc_in[...]

    attn_body(qvis_ref, q_ref, k_ref, v_ref, kh_ref, m_sc, l_sc, acc_sc, scale)

    @pl.when(j == nsteps - 1)
    def _():
        o_ref[...] = (acc_sc[...] / l_sc[...]).astype(o_ref.dtype)


def carry_kernel(own_ref, qvis_ref, q_ref, k_ref, v_ref, kh_ref, m_in, l_in, acc_in, m_ref, l_ref, acc_ref, *, scale):
    j = pl.program_id(0)

    @pl.when(j == 0)
    def _():
        m_ref[...] = m_in[...]
        l_ref[...] = l_in[...]
        acc_ref[...] = acc_in[...]

    attn_body(qvis_ref, q_ref, k_ref, v_ref, kh_ref, m_ref, l_ref, acc_ref, scale)


def attend_local(qvis, q, keys, values, key_hot, scale):
    nq, hd = q.shape
    tok = keys.shape[0]
    clip_count = qvis.shape[1]
    bk = math.gcd(tok, 1024)
    nsteps = tok // bk
    state = jax.ShapeDtypeStruct((nq, 128), jnp.float32)
    return pl.pallas_call(
        functools.partial(local_kernel, scale=scale),
        grid=(nsteps,),
        in_specs=[
            pl.BlockSpec((nq, clip_count), lambda j: (0, 0)),
            pl.BlockSpec((nq, hd), lambda j: (0, 0)),
            pl.BlockSpec((bk, hd), lambda j: (j, 0)),
            pl.BlockSpec((bk, hd), lambda j: (j, 0)),
            pl.BlockSpec((clip_count, bk), lambda j: (0, j)),
        ],
        out_specs=[
            pl.BlockSpec((nq, 128), lambda j: (0, 0)),
            pl.BlockSpec((nq, 128), lambda j: (0, 0)),
            pl.BlockSpec((nq, hd), lambda j: (0, 0)),
        ],
        out_shape=[state, state, jax.ShapeDtypeStruct((nq, hd), jnp.float32)],
        compiler_params=pltpu.CompilerParams(dimension_semantics=("arbitrary",)),
        cost_estimate=pl.CostEstimate(
            flops=4 * nq * tok * hd + 2 * nq * clip_count * tok,
            transcendentals=nq * tok,
            bytes_accessed=4 * tok * hd + 3 * nq * 512,
        ),
    )(qvis, q, keys, values, key_hot)


def attend_remote(own, qvis, q, kv_all, key_hot, carry, scale, tok, finalize):
    nq, hd = q.shape
    sources = kv_all.shape[0]
    clip_count = qvis.shape[1]
    bk = math.gcd(tok, 1024)
    sub = tok // bk
    nsteps = (sources - 1) * sub

    def src(j, o):
        return (o[0] + 1 + j // sub) % sources

    state_specs = [
        pl.BlockSpec((nq, 128), lambda j, o: (0, 0)),
        pl.BlockSpec((nq, 128), lambda j, o: (0, 0)),
        pl.BlockSpec((nq, hd), lambda j, o: (0, 0)),
    ]
    if finalize:
        kernel = functools.partial(remote_kernel, scale=scale, nsteps=nsteps)
        out_specs = pl.BlockSpec((nq, hd), lambda j, o: (0, 0))
        out_shape = jax.ShapeDtypeStruct((nq, hd), jnp.bfloat16)
        scratch = [
            pltpu.VMEM((nq, 128), jnp.float32),
            pltpu.VMEM((nq, 128), jnp.float32),
            pltpu.VMEM((nq, hd), jnp.float32),
        ]
    else:
        kernel = functools.partial(carry_kernel, scale=scale)
        out_specs = state_specs
        state = jax.ShapeDtypeStruct((nq, 128), jnp.float32)
        out_shape = [state, state, jax.ShapeDtypeStruct((nq, hd), jnp.float32)]
        scratch = []
    grid_spec = pltpu.PrefetchScalarGridSpec(
        num_scalar_prefetch=1,
        grid=(nsteps,),
        in_specs=[
            pl.BlockSpec((nq, clip_count), lambda j, o: (0, 0)),
            pl.BlockSpec((nq, hd), lambda j, o: (0, 0)),
            pl.BlockSpec((None, bk, hd), lambda j, o: (src(j, o), j % sub, 0)),
            pl.BlockSpec((None, bk, hd), lambda j, o: (src(j, o), sub + j % sub, 0)),
            pl.BlockSpec((None, clip_count, bk), lambda j, o: (src(j, o), 0, j % sub)),
        ] + state_specs,
        out_specs=out_specs,
        scratch_shapes=scratch,
    )
    return pl.pallas_call(
        kernel,
        grid_spec=grid_spec,
        out_shape=out_shape,
        compiler_params=pltpu.CompilerParams(dimension_semantics=("arbitrary",)),
        cost_estimate=pl.CostEstimate(
            flops=4 * nq * (sources - 1) * tok * hd + 2 * nq * clip_count * (sources - 1) * tok,
            transcendentals=nq * (sources - 1) * tok,
            bytes_accessed=kv_all.size * 2 + 3 * nq * 512,
        ),
    )(own, qvis, q, kv_all, kv_all, key_hot, *carry)


def per_device_body(activations, qkv_weight, out_weight, mod_table, clip_level, clip_of, visible):
    heads_here = qkv_weight.shape[2]
    head_size = qkv_weight.shape[3]
    clip_count = visible.shape[0]
    level_count = mod_table.shape[0]
    tok = clip_of.shape[0]
    clip_ids = lax.broadcasted_iota(jnp.int32, (1, clip_count), 1)
    level_ids = lax.broadcasted_iota(jnp.int32, (1, level_count), 1)
    tok_hot = clip_of[:, None] == clip_ids
    level_rows = jnp.sum(jnp.where(tok_hot, clip_level[None, :], 0), axis=1)
    level_hot = (level_rows[:, None] == level_ids).astype(jnp.float32)
    modulation = jnp.dot(level_hot, mod_table, precision=lax.Precision.HIGHEST)
    moduled = (activations.astype(jnp.float32) * (1.0 + modulation)).astype(jnp.bfloat16)
    qkv = jnp.einsum(
        "td,dchk->hctk", moduled, qkv_weight, preferred_element_type=jnp.float32
    ).astype(jnp.bfloat16)
    lane = head_size
    clip_rows = tok // lane
    pad_rows = -clip_rows % 8
    clip_slab = jnp.concatenate(
        [clip_of.astype(jnp.bfloat16).reshape(clip_rows, lane), jnp.zeros((pad_rows, lane), jnp.bfloat16)]
    )
    payload = jnp.concatenate(
        [qkv.reshape(heads_here, 3 * tok, lane), jnp.broadcast_to(clip_slab, (heads_here,) + clip_slab.shape)],
        axis=1,
    )
    exch = lax.all_to_all(payload, "yc", 0, 0, tiled=True)
    group_tok = heads_here * tok
    queries = exch[:, 0:tok].reshape(group_tok, lane)
    keys = exch[:, tok:2 * tok].reshape(group_tok, lane)
    values = exch[:, 2 * tok:3 * tok].reshape(group_tok, lane)
    clip_group = exch[:, 3 * tok:3 * tok + clip_rows].reshape(group_tok)
    sizes = [3 * group_tok // 4, group_tok // 4]
    starts = [0, sizes[0]]
    payloads = []
    for first, size in zip(starts, sizes):
        rows = size // lane
        payloads.append(
            jnp.concatenate(
                [
                    keys[first:first + size],
                    values[first:first + size],
                    clip_group[first:first + size].reshape(rows, lane),
                    jnp.zeros((-rows % 8, lane), jnp.bfloat16),
                ]
            )
        )
    query_hot = (clip_group.astype(jnp.int32)[:, None] == clip_ids).astype(jnp.float32)
    qvis = jnp.dot(query_hot, visible.astype(jnp.float32), precision=lax.Precision.HIGHEST).astype(jnp.bfloat16)
    score_scale = float(np.float32(1.0) / np.sqrt(np.float32(head_size)) * np.float32(math.log2(math.e)))
    local_hot = (clip_group.astype(jnp.int32)[None, :] == clip_ids[0][:, None]).astype(jnp.bfloat16)
    carry = attend_local(qvis, queries, keys, values, local_hot, score_scale)
    own = lax.axis_index("x").reshape(1).astype(jnp.int32)
    gathered = []
    for i in range(len(sizes)):
        gathered.append(lax.all_gather(payloads[i], "x", axis=0))
    for i, size in enumerate(sizes):
        kv_all = gathered[i]
        rows = size // lane
        key_clips = kv_all[:, 2 * size:2 * size + rows].reshape(kv_all.shape[0], size)
        key_hot = (key_clips.astype(jnp.int32)[:, None, :] == clip_ids[0][None, :, None]).astype(jnp.bfloat16)
        carry = attend_remote(own, qvis, queries, kv_all, key_hot, carry, score_scale, size, i == len(sizes) - 1)
    attended = carry
    back = lax.all_to_all(attended.reshape(heads_here, tok, lane), "yc", 0, 0, tiled=True)
    mixed = jnp.einsum(
        "hrd,hdo->ro", back, out_weight, preferred_element_type=jnp.float32
    ).astype(jnp.bfloat16)
    groups = lax.axis_size("head")
    parts = mixed.reshape(groups, mixed.shape[0] // groups, mixed.shape[1])
    parts = lax.all_to_all(parts, "head", 0, 0)
    return jnp.sum(parts.astype(jnp.float32), axis=0).astype(jnp.bfloat16)


def solution(mesh):
    ctx = mesh.shape["ctx"]
    heads = 4
    fine = Mesh(mesh.devices.reshape(ctx // heads, heads, mesh.shape["head"]), ("x", "yc", "head"))
    placed = (
        P(("x", "yc"), None),
        P(None, None, "head", None),
        P("head", None, None),
        P(),
        P(),
        P(("x", "yc")),
        P(),
    )
    return jax.shard_map(
        per_device_body, mesh=fine, in_specs=placed, out_specs=P(("x", "yc", "head"), None), check_vma=False
    )
```

```python
import functools
import math

import jax
import numpy as np
import jax.numpy as jnp
from jax import lax
from jax.experimental import pallas as pl
from jax.experimental.pallas import tpu as pltpu
from jax.sharding import Mesh, PartitionSpec as P


def attn_body(qvis_ref, q_ref, k_ref, v_ref, kh_ref, m_sc, l_sc, acc_sc, scale):
    lanes = m_sc.shape[1]
    allowed = jnp.dot(qvis_ref[...], kh_ref[...], preferred_element_type=jnp.float32)
    s = lax.dot_general(q_ref[...], k_ref[...], (((1,), (1,)), ((), ())), preferred_element_type=jnp.float32)
    bk = s.shape[1]
    s = jnp.where(allowed > 0.5, s * scale, -jnp.inf)
    m_old = m_sc[...]
    m_new = jnp.maximum(m_old, jnp.max(s, axis=1, keepdims=True))
    p = jnp.exp2(s - jnp.tile(m_new, (1, bk // lanes)))
    alpha = jnp.exp2(m_old - m_new)
    l_sc[...] = l_sc[...] * alpha + jnp.sum(p, axis=1, keepdims=True)
    acc_sc[...] = acc_sc[...] * alpha + jnp.dot(
        p.astype(jnp.bfloat16), v_ref[...], preferred_element_type=jnp.float32
    )
    m_sc[...] = m_new


def local_kernel(qvis_ref, q_ref, k_ref, v_ref, kh_ref, m_ref, l_ref, acc_ref, *, scale):
    j = pl.program_id(0)

    @pl.when(j == 0)
    def _():
        m_ref[...] = jnp.full(m_ref.shape, -1e30, jnp.float32)
        l_ref[...] = jnp.zeros(l_ref.shape, jnp.float32)
        acc_ref[...] = jnp.zeros(acc_ref.shape, jnp.float32)

    attn_body(qvis_ref, q_ref, k_ref, v_ref, kh_ref, m_ref, l_ref, acc_ref, scale)


def remote_kernel(own_ref, qvis_ref, q_ref, k_ref, v_ref, kh_ref, m_in, l_in, acc_in, o_ref, m_sc, l_sc, acc_sc, *, scale, nsteps):
    j = pl.program_id(0)

    @pl.when(j == 0)
    def _():
        m_sc[...] = m_in[...]
        l_sc[...] = l_in[...]
        acc_sc[...] = acc_in[...]

    attn_body(qvis_ref, q_ref, k_ref, v_ref, kh_ref, m_sc, l_sc, acc_sc, scale)

    @pl.when(j == nsteps - 1)
    def _():
        o_ref[...] = (acc_sc[...] / l_sc[...]).astype(o_ref.dtype)


def carry_kernel(own_ref, qvis_ref, q_ref, k_ref, v_ref, kh_ref, m_in, l_in, acc_in, m_ref, l_ref, acc_ref, *, scale):
    j = pl.program_id(0)

    @pl.when(j == 0)
    def _():
        m_ref[...] = m_in[...]
        l_ref[...] = l_in[...]
        acc_ref[...] = acc_in[...]

    attn_body(qvis_ref, q_ref, k_ref, v_ref, kh_ref, m_ref, l_ref, acc_ref, scale)


def attend_local(qvis, q, keys, values, key_hot, scale):
    nq, hd = q.shape
    tok = keys.shape[0]
    clip_count = qvis.shape[1]
    bk = math.gcd(tok, 1024)
    nsteps = tok // bk
    state = jax.ShapeDtypeStruct((nq, 128), jnp.float32)
    return pl.pallas_call(
        functools.partial(local_kernel, scale=scale),
        grid=(nsteps,),
        in_specs=[
            pl.BlockSpec((nq, clip_count), lambda j: (0, 0)),
            pl.BlockSpec((nq, hd), lambda j: (0, 0)),
            pl.BlockSpec((bk, hd), lambda j: (j, 0)),
            pl.BlockSpec((bk, hd), lambda j: (j, 0)),
            pl.BlockSpec((clip_count, bk), lambda j: (0, j)),
        ],
        out_specs=[
            pl.BlockSpec((nq, 128), lambda j: (0, 0)),
            pl.BlockSpec((nq, 128), lambda j: (0, 0)),
            pl.BlockSpec((nq, hd), lambda j: (0, 0)),
        ],
        out_shape=[state, state, jax.ShapeDtypeStruct((nq, hd), jnp.float32)],
        compiler_params=pltpu.CompilerParams(dimension_semantics=("arbitrary",)),
        cost_estimate=pl.CostEstimate(
            flops=4 * nq * tok * hd + 2 * nq * clip_count * tok,
            transcendentals=nq * tok,
            bytes_accessed=4 * tok * hd + 3 * nq * 512,
        ),
    )(qvis, q, keys, values, key_hot)


def attend_remote(own, qvis, q, kv_all, key_hot, carry, scale, tok, finalize):
    nq, hd = q.shape
    sources = kv_all.shape[0]
    clip_count = qvis.shape[1]
    bk = math.gcd(tok, 1024)
    sub = tok // bk
    nsteps = (sources - 1) * sub

    def src(j, o):
        return (o[0] + 1 + j // sub) % sources

    state_specs = [
        pl.BlockSpec((nq, 128), lambda j, o: (0, 0)),
        pl.BlockSpec((nq, 128), lambda j, o: (0, 0)),
        pl.BlockSpec((nq, hd), lambda j, o: (0, 0)),
    ]
    if finalize:
        kernel = functools.partial(remote_kernel, scale=scale, nsteps=nsteps)
        out_specs = pl.BlockSpec((nq, hd), lambda j, o: (0, 0))
        out_shape = jax.ShapeDtypeStruct((nq, hd), jnp.bfloat16)
        scratch = [
            pltpu.VMEM((nq, 128), jnp.float32),
            pltpu.VMEM((nq, 128), jnp.float32),
            pltpu.VMEM((nq, hd), jnp.float32),
        ]
    else:
        kernel = functools.partial(carry_kernel, scale=scale)
        out_specs = state_specs
        state = jax.ShapeDtypeStruct((nq, 128), jnp.float32)
        out_shape = [state, state, jax.ShapeDtypeStruct((nq, hd), jnp.float32)]
        scratch = []
    grid_spec = pltpu.PrefetchScalarGridSpec(
        num_scalar_prefetch=1,
        grid=(nsteps,),
        in_specs=[
            pl.BlockSpec((nq, clip_count), lambda j, o: (0, 0)),
            pl.BlockSpec((nq, hd), lambda j, o: (0, 0)),
            pl.BlockSpec((None, bk, hd), lambda j, o: (src(j, o), j % sub, 0)),
            pl.BlockSpec((None, bk, hd), lambda j, o: (src(j, o), sub + j % sub, 0)),
            pl.BlockSpec((None, clip_count, bk), lambda j, o: (src(j, o), 0, j % sub)),
        ] + state_specs,
        out_specs=out_specs,
        scratch_shapes=scratch,
    )
    return pl.pallas_call(
        kernel,
        grid_spec=grid_spec,
        out_shape=out_shape,
        compiler_params=pltpu.CompilerParams(dimension_semantics=("arbitrary",)),
        cost_estimate=pl.CostEstimate(
            flops=4 * nq * (sources - 1) * tok * hd + 2 * nq * clip_count * (sources - 1) * tok,
            transcendentals=nq * (sources - 1) * tok,
            bytes_accessed=kv_all.size * 2 + 3 * nq * 512,
        ),
    )(own, qvis, q, kv_all, kv_all, key_hot, *carry)


def per_device_body(activations, qkv_weight, out_weight, mod_table, clip_level, clip_of, visible):
    heads_here = qkv_weight.shape[2]
    head_size = qkv_weight.shape[3]
    clip_count = visible.shape[0]
    level_count = mod_table.shape[0]
    tok = clip_of.shape[0]
    clip_ids = lax.broadcasted_iota(jnp.int32, (1, clip_count), 1)
    level_ids = lax.broadcasted_iota(jnp.int32, (1, level_count), 1)
    tok_hot = clip_of[:, None] == clip_ids
    level_rows = jnp.sum(jnp.where(tok_hot, clip_level[None, :], 0), axis=1)
    level_hot = (level_rows[:, None] == level_ids).astype(jnp.float32)
    modulation = jnp.dot(level_hot, mod_table, precision=lax.Precision.HIGHEST)
    moduled = (activations.astype(jnp.float32) * (1.0 + modulation)).astype(jnp.bfloat16)
    qkv = jnp.einsum(
        "td,dchk->hctk", moduled, qkv_weight, preferred_element_type=jnp.float32
    ).astype(jnp.bfloat16)
    lane = head_size
    clip_rows = tok // lane
    pad_rows = -clip_rows % 8
    clip_slab = jnp.concatenate(
        [clip_of.astype(jnp.bfloat16).reshape(clip_rows, lane), jnp.zeros((pad_rows, lane), jnp.bfloat16)]
    )
    kv_part = jnp.concatenate(
        [qkv[:, 1:3].reshape(heads_here, 2 * tok, lane), jnp.broadcast_to(clip_slab, (heads_here,) + clip_slab.shape)],
        axis=1,
    )
    exch = lax.all_to_all(kv_part, "yc", 0, 0, tiled=True)
    q_part, exch = lax.optimization_barrier((qkv[:, 0], exch))
    exch_q = lax.all_to_all(q_part, "yc", 0, 0, tiled=True)
    group_tok = heads_here * tok
    queries = exch_q.reshape(group_tok, lane)
    keys = exch[:, 0:tok].reshape(group_tok, lane)
    values = exch[:, tok:2 * tok].reshape(group_tok, lane)
    clip_group = exch[:, 2 * tok:2 * tok + clip_rows].reshape(group_tok)
    halves = 2
    half_tok = group_tok // halves
    half_rows = half_tok // lane
    kv_pad = -half_rows % 8
    payloads = [
        jnp.concatenate(
            [
                keys[i * half_tok:(i + 1) * half_tok],
                values[i * half_tok:(i + 1) * half_tok],
                clip_group[i * half_tok:(i + 1) * half_tok].reshape(half_rows, lane),
                jnp.zeros((kv_pad, lane), jnp.bfloat16),
            ]
        )
        for i in range(halves)
    ]
    query_hot = (clip_group.astype(jnp.int32)[:, None] == clip_ids).astype(jnp.float32)
    qvis = jnp.dot(query_hot, visible.astype(jnp.float32), precision=lax.Precision.HIGHEST).astype(jnp.bfloat16)
    score_scale = float(np.float32(1.0) / np.sqrt(np.float32(head_size)) * np.float32(math.log2(math.e)))
    local_hot = (clip_group.astype(jnp.int32)[None, :] == clip_ids[0][:, None]).astype(jnp.bfloat16)
    carry = attend_local(qvis, queries, keys, values, local_hot, score_scale)
    own = lax.axis_index("x").reshape(1).astype(jnp.int32)
    gathered = []
    for i in range(halves):
        gathered.append(lax.all_gather(payloads[i], "x", axis=0))
    for i in range(halves):
        kv_all = gathered[i]
        key_clips = kv_all[:, 2 * half_tok:2 * half_tok + half_rows].reshape(kv_all.shape[0], half_tok)
        key_hot = (key_clips.astype(jnp.int32)[:, None, :] == clip_ids[0][None, :, None]).astype(jnp.bfloat16)
        carry = attend_remote(own, qvis, queries, kv_all, key_hot, carry, score_scale, half_tok, i == halves - 1)
    attended = carry
    back = lax.all_to_all(attended.reshape(heads_here, tok, lane), "yc", 0, 0, tiled=True)
    mixed = jnp.einsum(
        "hrd,hdo->ro", back, out_weight, preferred_element_type=jnp.float32
    ).astype(jnp.bfloat16)
    groups = lax.axis_size("head")
    parts = mixed.reshape(groups, mixed.shape[0] // groups, mixed.shape[1])
    parts = lax.all_to_all(parts, "head", 0, 0)
    return jnp.sum(parts.astype(jnp.float32), axis=0).astype(jnp.bfloat16)


def solution(mesh):
    ctx = mesh.shape["ctx"]
    heads = 4
    fine = Mesh(mesh.devices.reshape(ctx // heads, heads, mesh.shape["head"]), ("x", "yc", "head"))
    placed = (
        P(("x", "yc"), None),
        P(None, None, "head", None),
        P("head", None, None),
        P(),
        P(),
        P(("x", "yc")),
        P(),
    )
    return jax.shard_map(
        per_device_body, mesh=fine, in_specs=placed, out_specs=P(("x", "yc", "head"), None), check_vma=False
    )
```

```python
import functools
import math

import jax
import numpy as np
import jax.numpy as jnp
from jax import lax
from jax.experimental import pallas as pl
from jax.experimental.pallas import tpu as pltpu
from jax.sharding import Mesh, PartitionSpec as P


def attn_body(qvis_ref, q_ref, k_ref, v_ref, kh_ref, m_sc, l_sc, acc_sc, scale):
    lanes = m_sc.shape[1]
    allowed = jnp.dot(qvis_ref[...], kh_ref[...], preferred_element_type=jnp.float32)
    s = lax.dot_general(q_ref[...], k_ref[...], (((1,), (1,)), ((), ())), preferred_element_type=jnp.float32)
    bk = s.shape[1]
    s = jnp.where(allowed > 0.5, s * scale, -jnp.inf)
    m_old = m_sc[...]
    m_new = jnp.maximum(m_old, jnp.max(s, axis=1, keepdims=True))
    p = jnp.exp2(s - jnp.tile(m_new, (1, bk // lanes)))
    alpha = jnp.exp2(m_old - m_new)
    l_sc[...] = l_sc[...] * alpha + jnp.sum(p, axis=1, keepdims=True)
    acc_sc[...] = acc_sc[...] * alpha + jnp.dot(
        p.astype(jnp.bfloat16), v_ref[...], preferred_element_type=jnp.float32
    )
    m_sc[...] = m_new


def local_kernel(qvis_ref, q_ref, k_ref, v_ref, kh_ref, m_ref, l_ref, acc_ref, *, scale):
    j = pl.program_id(0)

    @pl.when(j == 0)
    def _():
        m_ref[...] = jnp.full(m_ref.shape, -1e30, jnp.float32)
        l_ref[...] = jnp.zeros(l_ref.shape, jnp.float32)
        acc_ref[...] = jnp.zeros(acc_ref.shape, jnp.float32)

    attn_body(qvis_ref, q_ref, k_ref, v_ref, kh_ref, m_ref, l_ref, acc_ref, scale)


def remote_kernel(own_ref, qvis_ref, q_ref, k_ref, v_ref, kh_ref, m_in, l_in, acc_in, o_ref, m_sc, l_sc, acc_sc, *, scale, nsteps):
    j = pl.program_id(0)

    @pl.when(j == 0)
    def _():
        m_sc[...] = m_in[...]
        l_sc[...] = l_in[...]
        acc_sc[...] = acc_in[...]

    attn_body(qvis_ref, q_ref, k_ref, v_ref, kh_ref, m_sc, l_sc, acc_sc, scale)

    @pl.when(j == nsteps - 1)
    def _():
        o_ref[...] = (acc_sc[...] / l_sc[...]).astype(o_ref.dtype)


def carry_kernel(own_ref, qvis_ref, q_ref, k_ref, v_ref, kh_ref, m_in, l_in, acc_in, m_ref, l_ref, acc_ref, *, scale):
    j = pl.program_id(0)

    @pl.when(j == 0)
    def _():
        m_ref[...] = m_in[...]
        l_ref[...] = l_in[...]
        acc_ref[...] = acc_in[...]

    attn_body(qvis_ref, q_ref, k_ref, v_ref, kh_ref, m_ref, l_ref, acc_ref, scale)


def attend_local(qvis, q, keys, values, key_hot, scale):
    nq, hd = q.shape
    tok = keys.shape[0]
    clip_count = qvis.shape[1]
    bk = math.gcd(tok, 1024)
    nsteps = tok // bk
    state = jax.ShapeDtypeStruct((nq, 128), jnp.float32)
    return pl.pallas_call(
        functools.partial(local_kernel, scale=scale),
        grid=(nsteps,),
        in_specs=[
            pl.BlockSpec((nq, clip_count), lambda j: (0, 0)),
            pl.BlockSpec((nq, hd), lambda j: (0, 0)),
            pl.BlockSpec((bk, hd), lambda j: (j, 0)),
            pl.BlockSpec((bk, hd), lambda j: (j, 0)),
            pl.BlockSpec((clip_count, bk), lambda j: (0, j)),
        ],
        out_specs=[
            pl.BlockSpec((nq, 128), lambda j: (0, 0)),
            pl.BlockSpec((nq, 128), lambda j: (0, 0)),
            pl.BlockSpec((nq, hd), lambda j: (0, 0)),
        ],
        out_shape=[state, state, jax.ShapeDtypeStruct((nq, hd), jnp.float32)],
        compiler_params=pltpu.CompilerParams(dimension_semantics=("arbitrary",)),
        cost_estimate=pl.CostEstimate(
            flops=4 * nq * tok * hd + 2 * nq * clip_count * tok,
            transcendentals=nq * tok,
            bytes_accessed=4 * tok * hd + 3 * nq * 512,
        ),
    )(qvis, q, keys, values, key_hot)


def attend_remote(own, qvis, q, kv_all, key_hot, carry, scale, finalize):
    nq, hd = q.shape
    sources, blocks, _, bk = key_hot.shape
    clip_count = qvis.shape[1]
    nsteps = (sources - 1) * blocks

    def src(j, o):
        return (o[0] + 1 + j // blocks) % sources

    state_specs = [
        pl.BlockSpec((nq, 128), lambda j, o: (0, 0)),
        pl.BlockSpec((nq, 128), lambda j, o: (0, 0)),
        pl.BlockSpec((nq, hd), lambda j, o: (0, 0)),
    ]
    if finalize:
        kernel = functools.partial(remote_kernel, scale=scale, nsteps=nsteps)
        out_specs = pl.BlockSpec((nq, hd), lambda j, o: (0, 0))
        out_shape = jax.ShapeDtypeStruct((nq, hd), jnp.bfloat16)
        scratch = [
            pltpu.VMEM((nq, 128), jnp.float32),
            pltpu.VMEM((nq, 128), jnp.float32),
            pltpu.VMEM((nq, hd), jnp.float32),
        ]
    else:
        kernel = functools.partial(carry_kernel, scale=scale)
        out_specs = state_specs
        state = jax.ShapeDtypeStruct((nq, 128), jnp.float32)
        out_shape = [state, state, jax.ShapeDtypeStruct((nq, hd), jnp.float32)]
        scratch = []
    grid_spec = pltpu.PrefetchScalarGridSpec(
        num_scalar_prefetch=1,
        grid=(nsteps,),
        in_specs=[
            pl.BlockSpec((nq, clip_count), lambda j, o: (0, 0)),
            pl.BlockSpec((nq, hd), lambda j, o: (0, 0)),
            pl.BlockSpec((None, None, bk, hd), lambda j, o: (src(j, o), j % blocks, 0, 0)),
            pl.BlockSpec((None, None, bk, hd), lambda j, o: (src(j, o), j % blocks, 1, 0)),
            pl.BlockSpec((None, None, clip_count, bk), lambda j, o: (src(j, o), j % blocks, 0, 0)),
        ] + state_specs,
        out_specs=out_specs,
        scratch_shapes=scratch,
    )
    keys_seen = (sources - 1) * blocks * bk
    return pl.pallas_call(
        kernel,
        grid_spec=grid_spec,
        out_shape=out_shape,
        compiler_params=pltpu.CompilerParams(dimension_semantics=("arbitrary",)),
        cost_estimate=pl.CostEstimate(
            flops=4 * nq * keys_seen * hd + 2 * nq * clip_count * keys_seen,
            transcendentals=nq * keys_seen,
            bytes_accessed=4 * keys_seen * hd + 3 * nq * 512,
        ),
    )(own, qvis, q, kv_all, kv_all, key_hot, *carry)


def per_device_body(activations, qkv_weight, out_weight, mod_table, clip_level, clip_of, visible):
    heads_here = qkv_weight.shape[2]
    head_size = qkv_weight.shape[3]
    clip_count = visible.shape[0]
    level_count = mod_table.shape[0]
    tok = clip_of.shape[0]
    clip_ids = lax.broadcasted_iota(jnp.int32, (1, clip_count), 1)
    level_ids = lax.broadcasted_iota(jnp.int32, (1, level_count), 1)
    tok_hot = clip_of[:, None] == clip_ids
    level_rows = jnp.sum(jnp.where(tok_hot, clip_level[None, :], 0), axis=1)
    level_hot = (level_rows[:, None] == level_ids).astype(jnp.float32)
    modulation = jnp.dot(level_hot, mod_table, precision=lax.Precision.HIGHEST)
    moduled = (activations.astype(jnp.float32) * (1.0 + modulation)).astype(jnp.bfloat16)
    qkv = jnp.einsum(
        "td,dchk->hctk", moduled, qkv_weight, preferred_element_type=jnp.float32
    ).astype(jnp.bfloat16)
    lane = head_size
    clip_rows = tok // lane
    pad_rows = -clip_rows % 8
    clip_slab = jnp.concatenate(
        [clip_of.astype(jnp.bfloat16).reshape(clip_rows, lane), jnp.zeros((pad_rows, lane), jnp.bfloat16)]
    )
    kv_part = jnp.concatenate(
        [qkv[:, 1:3].reshape(heads_here, 2 * tok, lane), jnp.broadcast_to(clip_slab, (heads_here,) + clip_slab.shape)],
        axis=1,
    )
    exch = lax.all_to_all(kv_part, "yc", 0, 0, tiled=True)
    q_part, exch = lax.optimization_barrier((qkv[:, 0], exch))
    exch_q = lax.all_to_all(q_part, "yc", 0, 0, tiled=True)
    group_tok = heads_here * tok
    queries = exch_q.reshape(group_tok, lane)
    keys = exch[:, 0:tok].reshape(group_tok, lane)
    values = exch[:, tok:2 * tok].reshape(group_tok, lane)
    clip_group = exch[:, 2 * tok:2 * tok + clip_rows].reshape(group_tok)
    query_hot = (clip_group.astype(jnp.int32)[:, None] == clip_ids).astype(jnp.float32)
    qvis = jnp.dot(query_hot, visible.astype(jnp.float32), precision=lax.Precision.HIGHEST).astype(jnp.bfloat16)
    score_scale = float(np.float32(1.0) / np.sqrt(np.float32(head_size)) * np.float32(math.log2(math.e)))
    local_hot = (clip_group.astype(jnp.int32)[None, :] == clip_ids[0][:, None]).astype(jnp.bfloat16)
    carry = attend_local(qvis, queries, keys, values, local_hot, score_scale)
    own = lax.axis_index("x").reshape(1).astype(jnp.int32)
    bounds = [(0, heads_here - 1), (heads_here - 1, heads_here)]
    gathered = []
    for lo, hi in bounds:
        gathered.append(lax.all_gather(exch[lo:hi], "x", axis=0))
    for i in range(len(bounds)):
        kv_all = gathered[i]
        key_clips = kv_all[:, :, 2 * tok:2 * tok + clip_rows].reshape(kv_all.shape[0], kv_all.shape[1], tok)
        key_hot = (key_clips.astype(jnp.int32)[:, :, None, :] == clip_ids[0][None, None, :, None]).astype(jnp.bfloat16)
        carry = attend_remote(own, qvis, queries, kv_all, key_hot, carry, score_scale, i == len(bounds) - 1)
    attended = carry
    back = lax.all_to_all(attended.reshape(heads_here, tok, lane), "yc", 0, 0, tiled=True)
    mixed = jnp.einsum(
        "hrd,hdo->ro", back, out_weight, preferred_element_type=jnp.float32
    ).astype(jnp.bfloat16)
    groups = lax.axis_size("head")
    parts = mixed.reshape(groups, mixed.shape[0] // groups, mixed.shape[1])
    parts = lax.all_to_all(parts, "head", 0, 0)
    return jnp.sum(parts.astype(jnp.float32), axis=0).astype(jnp.bfloat16)


def solution(mesh):
    ctx = mesh.shape["ctx"]
    heads = 4
    fine = Mesh(mesh.devices.reshape(ctx // heads, heads, mesh.shape["head"]), ("x", "yc", "head"))
    placed = (
        P(("x", "yc"), None),
        P(None, None, "head", None),
        P("head", None, None),
        P(),
        P(),
        P(("x", "yc")),
        P(),
    )
    return jax.shard_map(
        per_device_body, mesh=fine, in_specs=placed, out_specs=P(("x", "yc", "head"), None), check_vma=False
    )
```

```python
import functools
import math

import jax
import numpy as np
import jax.numpy as jnp
from jax import lax
from jax.experimental import pallas as pl
from jax.experimental.pallas import tpu as pltpu
from jax.sharding import Mesh, PartitionSpec as P


def attn_body(qvis_ref, q_ref, k_ref, v_ref, kh_ref, m_sc, l_sc, acc_sc, scale):
    lanes = m_sc.shape[1]
    allowed = jnp.dot(qvis_ref[...], kh_ref[...], preferred_element_type=jnp.float32)
    s = lax.dot_general(q_ref[...], k_ref[...], (((1,), (1,)), ((), ())), preferred_element_type=jnp.float32)
    bk = s.shape[1]
    s = jnp.where(allowed > 0.5, s * scale, -jnp.inf)
    m_old = m_sc[...]
    m_new = jnp.maximum(m_old, jnp.max(s, axis=1, keepdims=True))
    p = jnp.exp2(s - jnp.tile(m_new, (1, bk // lanes)))
    alpha = jnp.exp2(m_old - m_new)
    l_sc[...] = l_sc[...] * alpha + jnp.sum(p, axis=1, keepdims=True)
    acc_sc[...] = acc_sc[...] * alpha + jnp.dot(
        p.astype(jnp.bfloat16), v_ref[...], preferred_element_type=jnp.float32
    )
    m_sc[...] = m_new


def local_kernel(qvis_ref, q_ref, k_ref, v_ref, kh_ref, m_ref, l_ref, acc_ref, *, scale):
    j = pl.program_id(0)

    @pl.when(j == 0)
    def _():
        m_ref[...] = jnp.full(m_ref.shape, -1e30, jnp.float32)
        l_ref[...] = jnp.zeros(l_ref.shape, jnp.float32)
        acc_ref[...] = jnp.zeros(acc_ref.shape, jnp.float32)

    attn_body(qvis_ref, q_ref, k_ref, v_ref, kh_ref, m_ref, l_ref, acc_ref, scale)


def remote_kernel(own_ref, qvis_ref, q_ref, k_ref, v_ref, kh_ref, m_in, l_in, acc_in, o_ref, m_sc, l_sc, acc_sc, *, scale, nsteps):
    j = pl.program_id(0)

    @pl.when(j == 0)
    def _():
        m_sc[...] = m_in[...]
        l_sc[...] = l_in[...]
        acc_sc[...] = acc_in[...]

    attn_body(qvis_ref, q_ref, k_ref, v_ref, kh_ref, m_sc, l_sc, acc_sc, scale)

    @pl.when(j == nsteps - 1)
    def _():
        o_ref[...] = (acc_sc[...] / l_sc[...]).astype(o_ref.dtype)


def carry_kernel(own_ref, qvis_ref, q_ref, k_ref, v_ref, kh_ref, m_in, l_in, acc_in, m_ref, l_ref, acc_ref, *, scale):
    j = pl.program_id(0)

    @pl.when(j == 0)
    def _():
        m_ref[...] = m_in[...]
        l_ref[...] = l_in[...]
        acc_ref[...] = acc_in[...]

    attn_body(qvis_ref, q_ref, k_ref, v_ref, kh_ref, m_ref, l_ref, acc_ref, scale)


def attend_local(qvis, q, keys, values, key_hot, scale):
    nq, hd = q.shape
    tok = keys.shape[0]
    clip_count = qvis.shape[1]
    bk = math.gcd(tok, 1024)
    nsteps = tok // bk
    state = jax.ShapeDtypeStruct((nq, 128), jnp.float32)
    return pl.pallas_call(
        functools.partial(local_kernel, scale=scale),
        grid=(nsteps,),
        in_specs=[
            pl.BlockSpec((nq, clip_count), lambda j: (0, 0)),
            pl.BlockSpec((nq, hd), lambda j: (0, 0)),
            pl.BlockSpec((bk, hd), lambda j: (j, 0)),
            pl.BlockSpec((bk, hd), lambda j: (j, 0)),
            pl.BlockSpec((clip_count, bk), lambda j: (0, j)),
        ],
        out_specs=[
            pl.BlockSpec((nq, 128), lambda j: (0, 0)),
            pl.BlockSpec((nq, 128), lambda j: (0, 0)),
            pl.BlockSpec((nq, hd), lambda j: (0, 0)),
        ],
        out_shape=[state, state, jax.ShapeDtypeStruct((nq, hd), jnp.float32)],
        compiler_params=pltpu.CompilerParams(dimension_semantics=("arbitrary",)),
        cost_estimate=pl.CostEstimate(
            flops=4 * nq * tok * hd + 2 * nq * clip_count * tok,
            transcendentals=nq * tok,
            bytes_accessed=4 * tok * hd + 3 * nq * 512,
        ),
    )(qvis, q, keys, values, key_hot)


def attend_remote(own, qvis, q, kv_all, key_hot, carry, scale, finalize):
    nq, hd = q.shape
    sources, blocks, _, bk = key_hot.shape
    clip_count = qvis.shape[1]
    nsteps = (sources - 1) * blocks

    def src(j, o):
        return (o[0] + 1 + j // blocks) % sources

    state_specs = [
        pl.BlockSpec((nq, 128), lambda j, o: (0, 0)),
        pl.BlockSpec((nq, 128), lambda j, o: (0, 0)),
        pl.BlockSpec((nq, hd), lambda j, o: (0, 0)),
    ]
    if finalize:
        kernel = functools.partial(remote_kernel, scale=scale, nsteps=nsteps)
        out_specs = pl.BlockSpec((nq, hd), lambda j, o: (0, 0))
        out_shape = jax.ShapeDtypeStruct((nq, hd), jnp.bfloat16)
        scratch = [
            pltpu.VMEM((nq, 128), jnp.float32),
            pltpu.VMEM((nq, 128), jnp.float32),
            pltpu.VMEM((nq, hd), jnp.float32),
        ]
    else:
        kernel = functools.partial(carry_kernel, scale=scale)
        out_specs = state_specs
        state = jax.ShapeDtypeStruct((nq, 128), jnp.float32)
        out_shape = [state, state, jax.ShapeDtypeStruct((nq, hd), jnp.float32)]
        scratch = []
    grid_spec = pltpu.PrefetchScalarGridSpec(
        num_scalar_prefetch=1,
        grid=(nsteps,),
        in_specs=[
            pl.BlockSpec((nq, clip_count), lambda j, o: (0, 0)),
            pl.BlockSpec((nq, hd), lambda j, o: (0, 0)),
            pl.BlockSpec((None, None, bk, hd), lambda j, o: (src(j, o), j % blocks, 0, 0)),
            pl.BlockSpec((None, None, bk, hd), lambda j, o: (src(j, o), j % blocks, 1, 0)),
            pl.BlockSpec((None, None, clip_count, bk), lambda j, o: (src(j, o), j % blocks, 0, 0)),
        ] + state_specs,
        out_specs=out_specs,
        scratch_shapes=scratch,
    )
    keys_seen = (sources - 1) * blocks * bk
    return pl.pallas_call(
        kernel,
        grid_spec=grid_spec,
        out_shape=out_shape,
        compiler_params=pltpu.CompilerParams(dimension_semantics=("arbitrary",)),
        cost_estimate=pl.CostEstimate(
            flops=4 * nq * keys_seen * hd + 2 * nq * clip_count * keys_seen,
            transcendentals=nq * keys_seen,
            bytes_accessed=4 * keys_seen * hd + 3 * nq * 512,
        ),
    )(own, qvis, q, kv_all, kv_all, key_hot, *carry)


def per_device_body(activations, qkv_weight, out_weight, mod_table, clip_level, clip_of, visible):
    heads_here = qkv_weight.shape[2]
    head_size = qkv_weight.shape[3]
    clip_count = visible.shape[0]
    level_count = mod_table.shape[0]
    tok = clip_of.shape[0]
    clip_ids = lax.broadcasted_iota(jnp.int32, (1, clip_count), 1)
    level_ids = lax.broadcasted_iota(jnp.int32, (1, level_count), 1)
    tok_hot = clip_of[:, None] == clip_ids
    level_rows = jnp.sum(jnp.where(tok_hot, clip_level[None, :], 0), axis=1)
    level_hot = (level_rows[:, None] == level_ids).astype(jnp.float32)
    modulation = jnp.dot(level_hot, mod_table, precision=lax.Precision.HIGHEST)
    moduled = (activations.astype(jnp.float32) * (1.0 + modulation)).astype(jnp.bfloat16)
    qkv = jnp.einsum(
        "td,dchk->hctk", moduled, qkv_weight, preferred_element_type=jnp.float32
    ).astype(jnp.bfloat16)
    lane = head_size
    clip_rows = tok // lane
    pad_rows = -clip_rows % 8
    clip_slab = jnp.concatenate(
        [clip_of.astype(jnp.bfloat16).reshape(clip_rows, lane), jnp.zeros((pad_rows, lane), jnp.bfloat16)]
    )
    kv_part = jnp.concatenate(
        [qkv[:, 1:3].reshape(heads_here, 2 * tok, lane), jnp.broadcast_to(clip_slab, (heads_here,) + clip_slab.shape)],
        axis=1,
    )
    exch = lax.all_to_all(kv_part, "yc", 0, 0, tiled=True)
    q_part, exch = lax.optimization_barrier((qkv[:, 0], exch))
    exch_q = lax.all_to_all(q_part, "yc", 0, 0, tiled=True)
    group_tok = heads_here * tok
    queries = exch_q.reshape(group_tok, lane)
    keys = exch[:, 0:tok].reshape(group_tok, lane)
    values = exch[:, tok:2 * tok].reshape(group_tok, lane)
    clip_group = exch[:, 2 * tok:2 * tok + clip_rows].reshape(group_tok)
    query_hot = (clip_group.astype(jnp.int32)[:, None] == clip_ids).astype(jnp.float32)
    qvis = jnp.dot(query_hot, visible.astype(jnp.float32), precision=lax.Precision.HIGHEST).astype(jnp.bfloat16)
    score_scale = float(np.float32(1.0) / np.sqrt(np.float32(head_size)) * np.float32(math.log2(math.e)))
    local_hot = (clip_group.astype(jnp.int32)[None, :] == clip_ids[0][:, None]).astype(jnp.bfloat16)
    carry = attend_local(qvis, queries, keys, values, local_hot, score_scale)
    own = lax.axis_index("x").reshape(1).astype(jnp.int32)
    bounds = [(0, heads_here - 1), (heads_here - 1, heads_here)]
    gathered = []
    for lo, hi in bounds:
        gathered.append(lax.all_gather(exch[lo:hi], "x", axis=0))
    for i in range(len(bounds)):
        kv_all = gathered[i]
        key_clips = kv_all[:, :, 2 * tok:2 * tok + clip_rows].reshape(kv_all.shape[0], kv_all.shape[1], tok)
        key_hot = (key_clips.astype(jnp.int32)[:, :, None, :] == clip_ids[0][None, None, :, None]).astype(jnp.bfloat16)
        carry = attend_remote(own, qvis, queries, kv_all, key_hot, carry, score_scale, i == len(bounds) - 1)
    attended = carry
    back = lax.all_to_all(attended.reshape(heads_here, tok, lane), "yc", 0, 0, tiled=True)
    rows_all = jnp.transpose(back, (1, 0, 2)).reshape(tok, heads_here * head_size)
    ow = out_weight.reshape(heads_here * head_size, out_weight.shape[2])
    mixed = jnp.dot(rows_all, ow, preferred_element_type=jnp.float32).astype(jnp.bfloat16)
    groups = lax.axis_size("head")
    parts = mixed.reshape(groups, mixed.shape[0] // groups, mixed.shape[1])
    parts = lax.all_to_all(parts, "head", 0, 0)
    return jnp.sum(parts.astype(jnp.float32), axis=0).astype(jnp.bfloat16)


def solution(mesh):
    ctx = mesh.shape["ctx"]
    heads = 4
    fine = Mesh(mesh.devices.reshape(ctx // heads, heads, mesh.shape["head"]), ("x", "yc", "head"))
    placed = (
        P(("x", "yc"), None),
        P(None, None, "head", None),
        P("head", None, None),
        P(),
        P(),
        P(("x", "yc")),
        P(),
    )
    return jax.shard_map(
        per_device_body, mesh=fine, in_specs=placed, out_specs=P(("x", "yc", "head"), None), check_vma=False
    )
```

```python
import functools
import math

import jax
import numpy as np
import jax.numpy as jnp
from jax import lax
from jax.experimental import pallas as pl
from jax.experimental.pallas import tpu as pltpu
from jax.sharding import Mesh, PartitionSpec as P


def attn_body(qvis_ref, q_ref, k_ref, v_ref, kh_ref, m_sc, l_sc, acc_sc, scale):
    lanes = m_sc.shape[1]
    allowed = jnp.dot(qvis_ref[...], kh_ref[...], preferred_element_type=jnp.float32)
    s = lax.dot_general(q_ref[...], k_ref[...], (((1,), (1,)), ((), ())), preferred_element_type=jnp.float32)
    bk = s.shape[1]
    s = jnp.where(allowed > 0.5, s * scale, -jnp.inf)
    m_old = m_sc[...]
    m_new = jnp.maximum(m_old, jnp.max(s, axis=1, keepdims=True))
    p = jnp.exp2(s - jnp.tile(m_new, (1, bk // lanes)))
    alpha = jnp.exp2(m_old - m_new)
    l_sc[...] = l_sc[...] * alpha + jnp.sum(p, axis=1, keepdims=True)
    acc_sc[...] = acc_sc[...] * alpha + jnp.dot(
        p.astype(jnp.bfloat16), v_ref[...], preferred_element_type=jnp.float32
    )
    m_sc[...] = m_new


def local_kernel(qvis_ref, q_ref, k_ref, v_ref, kh_ref, m_ref, l_ref, acc_ref, *, scale):
    j = pl.program_id(0)

    @pl.when(j == 0)
    def _():
        m_ref[...] = jnp.full(m_ref.shape, -1e30, jnp.float32)
        l_ref[...] = jnp.zeros(l_ref.shape, jnp.float32)
        acc_ref[...] = jnp.zeros(acc_ref.shape, jnp.float32)

    attn_body(qvis_ref, q_ref, k_ref, v_ref, kh_ref, m_ref, l_ref, acc_ref, scale)


def remote_kernel(own_ref, qvis_ref, q_ref, k_ref, v_ref, kh_ref, m_in, l_in, acc_in, o_ref, m_sc, l_sc, acc_sc, *, scale, nsteps):
    j = pl.program_id(0)

    @pl.when(j == 0)
    def _():
        m_sc[...] = m_in[...]
        l_sc[...] = l_in[...]
        acc_sc[...] = acc_in[...]

    attn_body(qvis_ref, q_ref, k_ref, v_ref, kh_ref, m_sc, l_sc, acc_sc, scale)

    @pl.when(j == nsteps - 1)
    def _():
        o_ref[...] = (acc_sc[...] / l_sc[...]).astype(o_ref.dtype)


def carry_kernel(own_ref, qvis_ref, q_ref, k_ref, v_ref, kh_ref, m_in, l_in, acc_in, m_ref, l_ref, acc_ref, *, scale):
    j = pl.program_id(0)

    @pl.when(j == 0)
    def _():
        m_ref[...] = m_in[...]
        l_ref[...] = l_in[...]
        acc_ref[...] = acc_in[...]

    attn_body(qvis_ref, q_ref, k_ref, v_ref, kh_ref, m_ref, l_ref, acc_ref, scale)


def attend_local(qvis, q, keys, values, key_hot, scale):
    nq, hd = q.shape
    tok = keys.shape[0]
    clip_count = qvis.shape[1]
    bk = math.gcd(tok, 1024)
    nsteps = tok // bk
    state = jax.ShapeDtypeStruct((nq, 128), jnp.float32)
    return pl.pallas_call(
        functools.partial(local_kernel, scale=scale),
        grid=(nsteps,),
        in_specs=[
            pl.BlockSpec((nq, clip_count), lambda j: (0, 0)),
            pl.BlockSpec((nq, hd), lambda j: (0, 0)),
            pl.BlockSpec((bk, hd), lambda j: (j, 0)),
            pl.BlockSpec((bk, hd), lambda j: (j, 0)),
            pl.BlockSpec((clip_count, bk), lambda j: (0, j)),
        ],
        out_specs=[
            pl.BlockSpec((nq, 128), lambda j: (0, 0)),
            pl.BlockSpec((nq, 128), lambda j: (0, 0)),
            pl.BlockSpec((nq, hd), lambda j: (0, 0)),
        ],
        out_shape=[state, state, jax.ShapeDtypeStruct((nq, hd), jnp.float32)],
        compiler_params=pltpu.CompilerParams(dimension_semantics=("arbitrary",)),
        cost_estimate=pl.CostEstimate(
            flops=4 * nq * tok * hd + 2 * nq * clip_count * tok,
            transcendentals=nq * tok,
            bytes_accessed=4 * tok * hd + 3 * nq * 512,
        ),
    )(qvis, q, keys, values, key_hot)


def attend_remote(own, qvis, q, kv_all, key_hot, carry, scale, finalize):
    nq, hd = q.shape
    sources, blocks, _, bk = key_hot.shape
    clip_count = qvis.shape[1]
    nsteps = (sources - 1) * blocks

    def src(j, o):
        return (o[0] + 1 + j // blocks) % sources

    state_specs = [
        pl.BlockSpec((nq, 128), lambda j, o: (0, 0)),
        pl.BlockSpec((nq, 128), lambda j, o: (0, 0)),
        pl.BlockSpec((nq, hd), lambda j, o: (0, 0)),
    ]
    if finalize:
        kernel = functools.partial(remote_kernel, scale=scale, nsteps=nsteps)
        out_specs = pl.BlockSpec((nq, hd), lambda j, o: (0, 0))
        out_shape = jax.ShapeDtypeStruct((nq, hd), jnp.bfloat16)
        scratch = [
            pltpu.VMEM((nq, 128), jnp.float32),
            pltpu.VMEM((nq, 128), jnp.float32),
            pltpu.VMEM((nq, hd), jnp.float32),
        ]
    else:
        kernel = functools.partial(carry_kernel, scale=scale)
        out_specs = state_specs
        state = jax.ShapeDtypeStruct((nq, 128), jnp.float32)
        out_shape = [state, state, jax.ShapeDtypeStruct((nq, hd), jnp.float32)]
        scratch = []
    grid_spec = pltpu.PrefetchScalarGridSpec(
        num_scalar_prefetch=1,
        grid=(nsteps,),
        in_specs=[
            pl.BlockSpec((nq, clip_count), lambda j, o: (0, 0)),
            pl.BlockSpec((nq, hd), lambda j, o: (0, 0)),
            pl.BlockSpec((None, None, bk, hd), lambda j, o: (src(j, o), j % blocks, 0, 0)),
            pl.BlockSpec((None, None, bk, hd), lambda j, o: (src(j, o), j % blocks, 1, 0)),
            pl.BlockSpec((None, None, clip_count, bk), lambda j, o: (src(j, o), j % blocks, 0, 0)),
        ] + state_specs,
        out_specs=out_specs,
        scratch_shapes=scratch,
    )
    keys_seen = (sources - 1) * blocks * bk
    return pl.pallas_call(
        kernel,
        grid_spec=grid_spec,
        out_shape=out_shape,
        compiler_params=pltpu.CompilerParams(dimension_semantics=("arbitrary",)),
        cost_estimate=pl.CostEstimate(
            flops=4 * nq * keys_seen * hd + 2 * nq * clip_count * keys_seen,
            transcendentals=nq * keys_seen,
            bytes_accessed=4 * keys_seen * hd + 3 * nq * 512,
        ),
    )(own, qvis, q, kv_all, kv_all, key_hot, *carry)


def per_device_body(activations, qkv_weight, out_weight, mod_table, clip_level, clip_of, visible):
    heads_here = qkv_weight.shape[2]
    head_size = qkv_weight.shape[3]
    clip_count = visible.shape[0]
    level_count = mod_table.shape[0]
    tok = clip_of.shape[0]
    clip_ids = lax.broadcasted_iota(jnp.int32, (1, clip_count), 1)
    level_ids = lax.broadcasted_iota(jnp.int32, (1, level_count), 1)
    tok_hot = clip_of[:, None] == clip_ids
    level_rows = jnp.sum(jnp.where(tok_hot, clip_level[None, :], 0), axis=1)
    level_hot = (level_rows[:, None] == level_ids).astype(jnp.float32)
    modulation = jnp.dot(level_hot, mod_table, precision=lax.Precision.HIGHEST)
    moduled = (activations.astype(jnp.float32) * (1.0 + modulation)).astype(jnp.bfloat16)
    kv_proj = jnp.einsum(
        "td,dchk->hctk", moduled, qkv_weight[:, 1:3], preferred_element_type=jnp.float32
    ).astype(jnp.bfloat16)
    lane = head_size
    clip_rows = tok // lane
    pad_rows = -clip_rows % 8
    clip_slab = jnp.concatenate(
        [clip_of.astype(jnp.bfloat16).reshape(clip_rows, lane), jnp.zeros((pad_rows, lane), jnp.bfloat16)]
    )
    kv_part = jnp.concatenate(
        [kv_proj.reshape(heads_here, 2 * tok, lane), jnp.broadcast_to(clip_slab, (heads_here,) + clip_slab.shape)],
        axis=1,
    )
    exch = lax.all_to_all(kv_part, "yc", 0, 0, tiled=True)
    q_proj = jnp.einsum(
        "td,dhk->htk", moduled, qkv_weight[:, 0], preferred_element_type=jnp.float32
    ).astype(jnp.bfloat16)
    q_part, exch = lax.optimization_barrier((q_proj, exch))
    exch_q = lax.all_to_all(q_part, "yc", 0, 0, tiled=True)
    group_tok = heads_here * tok
    queries = exch_q.reshape(group_tok, lane)
    keys = exch[:, 0:tok].reshape(group_tok, lane)
    values = exch[:, tok:2 * tok].reshape(group_tok, lane)
    clip_group = exch[:, 2 * tok:2 * tok + clip_rows].reshape(group_tok)
    query_hot = (clip_group.astype(jnp.int32)[:, None] == clip_ids).astype(jnp.float32)
    qvis = jnp.dot(query_hot, visible.astype(jnp.float32), precision=lax.Precision.HIGHEST).astype(jnp.bfloat16)
    score_scale = float(np.float32(1.0) / np.sqrt(np.float32(head_size)) * np.float32(math.log2(math.e)))
    local_hot = (clip_group.astype(jnp.int32)[None, :] == clip_ids[0][:, None]).astype(jnp.bfloat16)
    carry = attend_local(qvis, queries, keys, values, local_hot, score_scale)
    own = lax.axis_index("x").reshape(1).astype(jnp.int32)
    bounds = [(0, heads_here - 1), (heads_here - 1, heads_here)]
    gathered = []
    for lo, hi in bounds:
        gathered.append(lax.all_gather(exch[lo:hi], "x", axis=0))
    for i in range(len(bounds)):
        kv_all = gathered[i]
        key_clips = kv_all[:, :, 2 * tok:2 * tok + clip_rows].reshape(kv_all.shape[0], kv_all.shape[1], tok)
        key_hot = (key_clips.astype(jnp.int32)[:, :, None, :] == clip_ids[0][None, None, :, None]).astype(jnp.bfloat16)
        carry = attend_remote(own, qvis, queries, kv_all, key_hot, carry, score_scale, i == len(bounds) - 1)
    attended = carry
    back = lax.all_to_all(attended.reshape(heads_here, tok, lane), "yc", 0, 0, tiled=True)
    rows_all = jnp.transpose(back, (1, 0, 2)).reshape(tok, heads_here * head_size)
    ow = out_weight.reshape(heads_here * head_size, out_weight.shape[2])
    mixed = jnp.dot(rows_all, ow, preferred_element_type=jnp.float32).astype(jnp.bfloat16)
    groups = lax.axis_size("head")
    parts = mixed.reshape(groups, mixed.shape[0] // groups, mixed.shape[1])
    parts = lax.all_to_all(parts, "head", 0, 0)
    return jnp.sum(parts.astype(jnp.float32), axis=0).astype(jnp.bfloat16)


def solution(mesh):
    ctx = mesh.shape["ctx"]
    heads = 4
    fine = Mesh(mesh.devices.reshape(ctx // heads, heads, mesh.shape["head"]), ("x", "yc", "head"))
    placed = (
        P(("x", "yc"), None),
        P(None, None, "head", None),
        P("head", None, None),
        P(),
        P(),
        P(("x", "yc")),
        P(),
    )
    return jax.shard_map(
        per_device_body, mesh=fine, in_specs=placed, out_specs=P(("x", "yc", "head"), None), check_vma=False
    )
```

```python
import functools
import math

import jax
import numpy as np
import jax.numpy as jnp
from jax import lax
from jax.experimental import pallas as pl
from jax.experimental.pallas import tpu as pltpu
from jax.sharding import Mesh, PartitionSpec as P


def attn_body(qvis_ref, q_ref, k_ref, v_ref, kh_ref, m_sc, l_sc, acc_sc, scale):
    lanes = m_sc.shape[1]
    allowed = jnp.dot(qvis_ref[...], kh_ref[...], preferred_element_type=jnp.float32)
    s = lax.dot_general(q_ref[...], k_ref[...], (((1,), (1,)), ((), ())), preferred_element_type=jnp.float32)
    bk = s.shape[1]
    s = jnp.where(allowed > 0.5, s * scale, -jnp.inf)
    m_old = m_sc[...]
    m_new = jnp.maximum(m_old, jnp.max(s, axis=1, keepdims=True))
    p = jnp.exp2(s - jnp.tile(m_new, (1, bk // lanes)))
    alpha = jnp.exp2(m_old - m_new)
    l_sc[...] = l_sc[...] * alpha + jnp.sum(p, axis=1, keepdims=True)
    acc_sc[...] = acc_sc[...] * alpha + jnp.dot(
        p.astype(jnp.bfloat16), v_ref[...], preferred_element_type=jnp.float32
    )
    m_sc[...] = m_new


def local_kernel(qvis_ref, q_ref, k_ref, v_ref, kh_ref, m_ref, l_ref, acc_ref, *, scale):
    j = pl.program_id(0)

    @pl.when(j == 0)
    def _():
        m_ref[...] = jnp.full(m_ref.shape, -1e30, jnp.float32)
        l_ref[...] = jnp.zeros(l_ref.shape, jnp.float32)
        acc_ref[...] = jnp.zeros(acc_ref.shape, jnp.float32)

    attn_body(qvis_ref, q_ref, k_ref, v_ref, kh_ref, m_ref, l_ref, acc_ref, scale)


def remote_kernel(own_ref, qvis_ref, q_ref, k_ref, v_ref, kh_ref, m_in, l_in, acc_in, o_ref, m_sc, l_sc, acc_sc, *, scale, nsteps):
    j = pl.program_id(0)

    @pl.when(j == 0)
    def _():
        m_sc[...] = m_in[...]
        l_sc[...] = l_in[...]
        acc_sc[...] = acc_in[...]

    attn_body(qvis_ref, q_ref, k_ref, v_ref, kh_ref, m_sc, l_sc, acc_sc, scale)

    @pl.when(j == nsteps - 1)
    def _():
        o_ref[...] = (acc_sc[...] / l_sc[...]).astype(o_ref.dtype)


def carry_kernel(own_ref, qvis_ref, q_ref, k_ref, v_ref, kh_ref, m_in, l_in, acc_in, m_ref, l_ref, acc_ref, *, scale):
    j = pl.program_id(0)

    @pl.when(j == 0)
    def _():
        m_ref[...] = m_in[...]
        l_ref[...] = l_in[...]
        acc_ref[...] = acc_in[...]

    attn_body(qvis_ref, q_ref, k_ref, v_ref, kh_ref, m_ref, l_ref, acc_ref, scale)


def attend_local(qvis, q, keys, values, key_hot, scale):
    nq, hd = q.shape
    tok = keys.shape[0]
    clip_count = qvis.shape[1]
    bk = math.gcd(tok, 1024)
    nsteps = tok // bk
    state = jax.ShapeDtypeStruct((nq, 128), jnp.float32)
    return pl.pallas_call(
        functools.partial(local_kernel, scale=scale),
        grid=(nsteps,),
        in_specs=[
            pl.BlockSpec((nq, clip_count), lambda j: (0, 0)),
            pl.BlockSpec((nq, hd), lambda j: (0, 0)),
            pl.BlockSpec((bk, hd), lambda j: (j, 0)),
            pl.BlockSpec((bk, hd), lambda j: (j, 0)),
            pl.BlockSpec((clip_count, bk), lambda j: (0, j)),
        ],
        out_specs=[
            pl.BlockSpec((nq, 128), lambda j: (0, 0)),
            pl.BlockSpec((nq, 128), lambda j: (0, 0)),
            pl.BlockSpec((nq, hd), lambda j: (0, 0)),
        ],
        out_shape=[state, state, jax.ShapeDtypeStruct((nq, hd), jnp.float32)],
        compiler_params=pltpu.CompilerParams(dimension_semantics=("arbitrary",)),
        cost_estimate=pl.CostEstimate(
            flops=4 * nq * tok * hd + 2 * nq * clip_count * tok,
            transcendentals=nq * tok,
            bytes_accessed=4 * tok * hd + 3 * nq * 512,
        ),
    )(qvis, q, keys, values, key_hot)


def attend_remote(own, qvis, q, kv_all, key_hot, carry, scale, finalize):
    nq, hd = q.shape
    sources, blocks, _, bk = key_hot.shape
    clip_count = qvis.shape[1]
    nsteps = (sources - 1) * blocks

    def src(j, o):
        return (o[0] + 1 + j // blocks) % sources

    state_specs = [
        pl.BlockSpec((nq, 128), lambda j, o: (0, 0)),
        pl.BlockSpec((nq, 128), lambda j, o: (0, 0)),
        pl.BlockSpec((nq, hd), lambda j, o: (0, 0)),
    ]
    if finalize:
        kernel = functools.partial(remote_kernel, scale=scale, nsteps=nsteps)
        out_specs = pl.BlockSpec((nq, hd), lambda j, o: (0, 0))
        out_shape = jax.ShapeDtypeStruct((nq, hd), jnp.bfloat16)
        scratch = [
            pltpu.VMEM((nq, 128), jnp.float32),
            pltpu.VMEM((nq, 128), jnp.float32),
            pltpu.VMEM((nq, hd), jnp.float32),
        ]
    else:
        kernel = functools.partial(carry_kernel, scale=scale)
        out_specs = state_specs
        state = jax.ShapeDtypeStruct((nq, 128), jnp.float32)
        out_shape = [state, state, jax.ShapeDtypeStruct((nq, hd), jnp.float32)]
        scratch = []
    grid_spec = pltpu.PrefetchScalarGridSpec(
        num_scalar_prefetch=1,
        grid=(nsteps,),
        in_specs=[
            pl.BlockSpec((nq, clip_count), lambda j, o: (0, 0)),
            pl.BlockSpec((nq, hd), lambda j, o: (0, 0)),
            pl.BlockSpec((None, None, bk, hd), lambda j, o: (src(j, o), j % blocks, 0, 0)),
            pl.BlockSpec((None, None, bk, hd), lambda j, o: (src(j, o), j % blocks, 1, 0)),
            pl.BlockSpec((None, None, clip_count, bk), lambda j, o: (src(j, o), j % blocks, 0, 0)),
        ] + state_specs,
        out_specs=out_specs,
        scratch_shapes=scratch,
    )
    keys_seen = (sources - 1) * blocks * bk
    return pl.pallas_call(
        kernel,
        grid_spec=grid_spec,
        out_shape=out_shape,
        compiler_params=pltpu.CompilerParams(dimension_semantics=("arbitrary",)),
        cost_estimate=pl.CostEstimate(
            flops=4 * nq * keys_seen * hd + 2 * nq * clip_count * keys_seen,
            transcendentals=nq * keys_seen,
            bytes_accessed=4 * keys_seen * hd + 3 * nq * 512,
        ),
    )(own, qvis, q, kv_all, kv_all, key_hot, *carry)


def per_device_body(activations, qkv_weight, out_weight, mod_table, clip_level, clip_of, visible):
    heads_here = qkv_weight.shape[2]
    head_size = qkv_weight.shape[3]
    clip_count = visible.shape[0]
    level_count = mod_table.shape[0]
    tok = clip_of.shape[0]
    clip_ids = lax.broadcasted_iota(jnp.int32, (1, clip_count), 1)
    level_ids = lax.broadcasted_iota(jnp.int32, (1, level_count), 1)
    tok_hot = clip_of[:, None] == clip_ids
    level_rows = jnp.sum(jnp.where(tok_hot, clip_level[None, :], 0), axis=1)
    level_hot = (level_rows[:, None] == level_ids).astype(jnp.float32)
    modulation = jnp.dot(level_hot, mod_table, precision=lax.Precision.HIGHEST)
    moduled = (activations.astype(jnp.float32) * (1.0 + modulation)).astype(jnp.bfloat16)
    kv_proj = jnp.einsum(
        "td,dchk->hctk", moduled, qkv_weight[:, 1:3], preferred_element_type=jnp.float32
    ).astype(jnp.bfloat16)
    lane = head_size
    clip_rows = tok // lane
    pad_rows = -clip_rows % 8
    clip_slab = jnp.concatenate(
        [clip_of.astype(jnp.bfloat16).reshape(clip_rows, lane), jnp.zeros((pad_rows, lane), jnp.bfloat16)]
    )
    kv_part = jnp.concatenate(
        [kv_proj.reshape(heads_here, 2 * tok, lane), jnp.broadcast_to(clip_slab, (heads_here,) + clip_slab.shape)],
        axis=1,
    )
    exch = lax.all_to_all(kv_part, "yc", 0, 0, tiled=True)
    q_proj = jnp.einsum(
        "td,dhk->htk", moduled, qkv_weight[:, 0], preferred_element_type=jnp.float32
    ).astype(jnp.bfloat16)
    q_part, exch = lax.optimization_barrier((q_proj, exch))
    exch_q = lax.all_to_all(q_part, "yc", 0, 0, tiled=True)
    group_tok = heads_here * tok
    queries = exch_q.reshape(group_tok, lane)
    keys = exch[:, 0:tok].reshape(group_tok, lane)
    values = exch[:, tok:2 * tok].reshape(group_tok, lane)
    clip_group = exch[:, 2 * tok:2 * tok + clip_rows].reshape(group_tok)
    query_hot = (clip_group.astype(jnp.int32)[:, None] == clip_ids).astype(jnp.float32)
    qvis = jnp.dot(query_hot, visible.astype(jnp.float32), precision=lax.Precision.HIGHEST).astype(jnp.bfloat16)
    score_scale = float(np.float32(1.0) / np.sqrt(np.float32(head_size)) * np.float32(math.log2(math.e)))
    local_hot = (clip_group.astype(jnp.int32)[None, :] == clip_ids[0][:, None]).astype(jnp.bfloat16)
    carry = attend_local(qvis, queries, keys, values, local_hot, score_scale)
    own = lax.axis_index("x").reshape(1).astype(jnp.int32)
    bounds = [(0, heads_here - 1), (heads_here - 1, heads_here)]
    gathered = []
    for lo, hi in bounds:
        gathered.append(lax.all_gather(exch[lo:hi], "x", axis=0))
    for i in range(len(bounds)):
        kv_all = gathered[i]
        key_clips = kv_all[:, :, 2 * tok:2 * tok + clip_rows].reshape(kv_all.shape[0], kv_all.shape[1], tok)
        key_hot = (key_clips.astype(jnp.int32)[:, :, None, :] == clip_ids[0][None, None, :, None]).astype(jnp.bfloat16)
        carry = attend_remote(own, qvis, queries, kv_all, key_hot, carry, score_scale, i == len(bounds) - 1)
    attended = carry
    back = lax.all_to_all(attended.reshape(heads_here, tok, lane), "yc", 0, 0, tiled=True)
    rows_all = jnp.transpose(back, (1, 0, 2)).reshape(tok, heads_here * head_size)
    ow = out_weight.reshape(heads_here * head_size, out_weight.shape[2])
    groups = lax.axis_size("head")
    width = ow.shape[1] // 2
    outs = []
    for c in range(2):
        mixed = jnp.dot(
            rows_all, ow[:, c * width:(c + 1) * width], preferred_element_type=jnp.float32
        ).astype(jnp.bfloat16)
        parts = mixed.reshape(groups, mixed.shape[0] // groups, width)
        parts = lax.all_to_all(parts, "head", 0, 0)
        outs.append(jnp.sum(parts.astype(jnp.float32), axis=0).astype(jnp.bfloat16))
    return jnp.concatenate(outs, axis=1)


def solution(mesh):
    ctx = mesh.shape["ctx"]
    heads = 4
    fine = Mesh(mesh.devices.reshape(ctx // heads, heads, mesh.shape["head"]), ("x", "yc", "head"))
    placed = (
        P(("x", "yc"), None),
        P(None, None, "head", None),
        P("head", None, None),
        P(),
        P(),
        P(("x", "yc")),
        P(),
    )
    return jax.shard_map(
        per_device_body, mesh=fine, in_specs=placed, out_specs=P(("x", "yc", "head"), None), check_vma=False
    )
```

```python
import functools
import math

import jax
import numpy as np
import jax.numpy as jnp
from jax import lax
from jax.experimental import pallas as pl
from jax.experimental.pallas import tpu as pltpu
from jax.sharding import Mesh, PartitionSpec as P


def attn_body(qvis_ref, q_ref, k_ref, v_ref, kh_ref, m_sc, l_sc, acc_sc, scale):
    lanes = m_sc.shape[1]
    allowed = jnp.dot(qvis_ref[...], kh_ref[...], preferred_element_type=jnp.float32)
    s = lax.dot_general(q_ref[...], k_ref[...], (((1,), (1,)), ((), ())), preferred_element_type=jnp.float32)
    bk = s.shape[1]
    s = jnp.where(allowed > 0.5, s * scale, -jnp.inf)
    m_old = m_sc[...]
    m_new = jnp.maximum(m_old, jnp.max(s, axis=1, keepdims=True))
    p = jnp.exp2(s - jnp.tile(m_new, (1, bk // lanes)))
    alpha = jnp.exp2(m_old - m_new)
    l_sc[...] = l_sc[...] * alpha + jnp.sum(p, axis=1, keepdims=True)
    acc_sc[...] = acc_sc[...] * alpha + jnp.dot(
        p.astype(jnp.bfloat16), v_ref[...], preferred_element_type=jnp.float32
    )
    m_sc[...] = m_new


def local_kernel(qvis_ref, q_ref, k_ref, v_ref, kh_ref, m_ref, l_ref, acc_ref, *, scale):
    j = pl.program_id(0)

    @pl.when(j == 0)
    def _():
        m_ref[...] = jnp.full(m_ref.shape, -1e30, jnp.float32)
        l_ref[...] = jnp.zeros(l_ref.shape, jnp.float32)
        acc_ref[...] = jnp.zeros(acc_ref.shape, jnp.float32)

    attn_body(qvis_ref, q_ref, k_ref, v_ref, kh_ref, m_ref, l_ref, acc_ref, scale)


def remote_kernel(own_ref, qvis_ref, q_ref, k_ref, v_ref, kh_ref, m_in, l_in, acc_in, o_ref, m_sc, l_sc, acc_sc, *, scale, nsteps):
    j = pl.program_id(0)

    @pl.when(j == 0)
    def _():
        m_sc[...] = m_in[...]
        l_sc[...] = l_in[...]
        acc_sc[...] = acc_in[...]

    attn_body(qvis_ref, q_ref, k_ref, v_ref, kh_ref, m_sc, l_sc, acc_sc, scale)

    @pl.when(j == nsteps - 1)
    def _():
        o_ref[...] = (acc_sc[...] / l_sc[...]).astype(o_ref.dtype)


def carry_kernel(own_ref, qvis_ref, q_ref, k_ref, v_ref, kh_ref, m_in, l_in, acc_in, m_ref, l_ref, acc_ref, *, scale):
    j = pl.program_id(0)

    @pl.when(j == 0)
    def _():
        m_ref[...] = m_in[...]
        l_ref[...] = l_in[...]
        acc_ref[...] = acc_in[...]

    attn_body(qvis_ref, q_ref, k_ref, v_ref, kh_ref, m_ref, l_ref, acc_ref, scale)


def attend_local(qvis, q, keys, values, key_hot, scale):
    nq, hd = q.shape
    tok = keys.shape[0]
    clip_count = qvis.shape[1]
    bk = math.gcd(tok, 1024)
    nsteps = tok // bk
    state = jax.ShapeDtypeStruct((nq, 128), jnp.float32)
    return pl.pallas_call(
        functools.partial(local_kernel, scale=scale),
        grid=(nsteps,),
        in_specs=[
            pl.BlockSpec((nq, clip_count), lambda j: (0, 0)),
            pl.BlockSpec((nq, hd), lambda j: (0, 0)),
            pl.BlockSpec((bk, hd), lambda j: (j, 0)),
            pl.BlockSpec((bk, hd), lambda j: (j, 0)),
            pl.BlockSpec((clip_count, bk), lambda j: (0, j)),
        ],
        out_specs=[
            pl.BlockSpec((nq, 128), lambda j: (0, 0)),
            pl.BlockSpec((nq, 128), lambda j: (0, 0)),
            pl.BlockSpec((nq, hd), lambda j: (0, 0)),
        ],
        out_shape=[state, state, jax.ShapeDtypeStruct((nq, hd), jnp.float32)],
        compiler_params=pltpu.CompilerParams(dimension_semantics=("arbitrary",)),
        cost_estimate=pl.CostEstimate(
            flops=4 * nq * tok * hd + 2 * nq * clip_count * tok,
            transcendentals=nq * tok,
            bytes_accessed=4 * tok * hd + 3 * nq * 512,
        ),
    )(qvis, q, keys, values, key_hot)


def attend_remote(own, qvis, q, kv_all, key_hot, carry, scale, finalize):
    nq, hd = q.shape
    sources, blocks, _, bk = key_hot.shape
    clip_count = qvis.shape[1]
    nsteps = (sources - 1) * blocks

    def src(j, o):
        return (o[0] + 1 + j // blocks) % sources

    state_specs = [
        pl.BlockSpec((nq, 128), lambda j, o: (0, 0)),
        pl.BlockSpec((nq, 128), lambda j, o: (0, 0)),
        pl.BlockSpec((nq, hd), lambda j, o: (0, 0)),
    ]
    if finalize:
        kernel = functools.partial(remote_kernel, scale=scale, nsteps=nsteps)
        out_specs = pl.BlockSpec((nq, hd), lambda j, o: (0, 0))
        out_shape = jax.ShapeDtypeStruct((nq, hd), jnp.bfloat16)
        scratch = [
            pltpu.VMEM((nq, 128), jnp.float32),
            pltpu.VMEM((nq, 128), jnp.float32),
            pltpu.VMEM((nq, hd), jnp.float32),
        ]
    else:
        kernel = functools.partial(carry_kernel, scale=scale)
        out_specs = state_specs
        state = jax.ShapeDtypeStruct((nq, 128), jnp.float32)
        out_shape = [state, state, jax.ShapeDtypeStruct((nq, hd), jnp.float32)]
        scratch = []
    grid_spec = pltpu.PrefetchScalarGridSpec(
        num_scalar_prefetch=1,
        grid=(nsteps,),
        in_specs=[
            pl.BlockSpec((nq, clip_count), lambda j, o: (0, 0)),
            pl.BlockSpec((nq, hd), lambda j, o: (0, 0)),
            pl.BlockSpec((None, None, bk, hd), lambda j, o: (src(j, o), j % blocks, 0, 0)),
            pl.BlockSpec((None, None, bk, hd), lambda j, o: (src(j, o), j % blocks, 1, 0)),
            pl.BlockSpec((None, None, clip_count, bk), lambda j, o: (src(j, o), j % blocks, 0, 0)),
        ] + state_specs,
        out_specs=out_specs,
        scratch_shapes=scratch,
    )
    keys_seen = (sources - 1) * blocks * bk
    return pl.pallas_call(
        kernel,
        grid_spec=grid_spec,
        out_shape=out_shape,
        compiler_params=pltpu.CompilerParams(dimension_semantics=("arbitrary",)),
        cost_estimate=pl.CostEstimate(
            flops=4 * nq * keys_seen * hd + 2 * nq * clip_count * keys_seen,
            transcendentals=nq * keys_seen,
            bytes_accessed=4 * keys_seen * hd + 3 * nq * 512,
        ),
    )(own, qvis, q, kv_all, kv_all, key_hot, *carry)


def per_device_body(activations, qkv_weight, out_weight, mod_table, clip_level, clip_of, visible):
    heads_here = qkv_weight.shape[2]
    head_size = qkv_weight.shape[3]
    clip_count = visible.shape[0]
    level_count = mod_table.shape[0]
    tok = clip_of.shape[0]
    clip_ids = lax.broadcasted_iota(jnp.int32, (1, clip_count), 1)
    level_ids = lax.broadcasted_iota(jnp.int32, (1, level_count), 1)
    tok_hot = clip_of[:, None] == clip_ids
    level_rows = jnp.sum(jnp.where(tok_hot, clip_level[None, :], 0), axis=1)
    level_hot = (level_rows[:, None] == level_ids).astype(jnp.float32)
    modulation = jnp.dot(level_hot, mod_table, precision=lax.Precision.HIGHEST)
    moduled = (activations.astype(jnp.float32) * (1.0 + modulation)).astype(jnp.bfloat16)
    k_proj, v_proj = [
        jnp.einsum("td,dhk->htk", moduled, qkv_weight[:, c], preferred_element_type=jnp.float32).astype(jnp.bfloat16)
        for c in (1, 2)
    ]
    lane = head_size
    clip_rows = tok // lane
    pad_rows = -clip_rows % 8
    clip_slab = jnp.concatenate(
        [clip_of.astype(jnp.bfloat16).reshape(clip_rows, lane), jnp.zeros((pad_rows, lane), jnp.bfloat16)]
    )
    kv_part = jnp.concatenate(
        [k_proj, v_proj, jnp.broadcast_to(clip_slab, (heads_here,) + clip_slab.shape)],
        axis=1,
    )
    exch = lax.all_to_all(kv_part, "yc", 0, 0, tiled=True)
    q_proj = jnp.einsum(
        "td,dhk->htk", moduled, qkv_weight[:, 0], preferred_element_type=jnp.float32
    ).astype(jnp.bfloat16)
    q_part, exch = lax.optimization_barrier((q_proj, exch))
    exch_q = lax.all_to_all(q_part, "yc", 0, 0, tiled=True)
    group_tok = heads_here * tok
    queries = exch_q.reshape(group_tok, lane)
    keys = exch[:, 0:tok].reshape(group_tok, lane)
    values = exch[:, tok:2 * tok].reshape(group_tok, lane)
    clip_group = exch[:, 2 * tok:2 * tok + clip_rows].reshape(group_tok)
    query_hot = (clip_group.astype(jnp.int32)[:, None] == clip_ids).astype(jnp.float32)
    qvis = jnp.dot(query_hot, visible.astype(jnp.float32), precision=lax.Precision.HIGHEST).astype(jnp.bfloat16)
    score_scale = float(np.float32(1.0) / np.sqrt(np.float32(head_size)) * np.float32(math.log2(math.e)))
    local_hot = (clip_group.astype(jnp.int32)[None, :] == clip_ids[0][:, None]).astype(jnp.bfloat16)
    carry = attend_local(qvis, queries, keys, values, local_hot, score_scale)
    own = lax.axis_index("x").reshape(1).astype(jnp.int32)
    bounds = [(0, heads_here - 1), (heads_here - 1, heads_here)]
    gathered = []
    for lo, hi in bounds:
        gathered.append(lax.all_gather(exch[lo:hi], "x", axis=0))
    for i in range(len(bounds)):
        kv_all = gathered[i]
        key_clips = kv_all[:, :, 2 * tok:2 * tok + clip_rows].reshape(kv_all.shape[0], kv_all.shape[1], tok)
        key_hot = (key_clips.astype(jnp.int32)[:, :, None, :] == clip_ids[0][None, None, :, None]).astype(jnp.bfloat16)
        carry = attend_remote(own, qvis, queries, kv_all, key_hot, carry, score_scale, i == len(bounds) - 1)
    attended = carry
    back = lax.all_to_all(attended.reshape(heads_here, tok, lane), "yc", 0, 0, tiled=True)
    rows_all = jnp.transpose(back, (1, 0, 2)).reshape(tok, heads_here * head_size)
    ow = out_weight.reshape(heads_here * head_size, out_weight.shape[2])
    mixed = jnp.dot(rows_all, ow, preferred_element_type=jnp.float32).astype(jnp.bfloat16)
    groups = lax.axis_size("head")
    parts = mixed.reshape(groups, mixed.shape[0] // groups, mixed.shape[1])
    parts = lax.all_to_all(parts, "head", 0, 0)
    return jnp.sum(parts.astype(jnp.float32), axis=0).astype(jnp.bfloat16)


def solution(mesh):
    ctx = mesh.shape["ctx"]
    heads = 4
    fine = Mesh(mesh.devices.reshape(ctx // heads, heads, mesh.shape["head"]), ("x", "yc", "head"))
    placed = (
        P(("x", "yc"), None),
        P(None, None, "head", None),
        P("head", None, None),
        P(),
        P(),
        P(("x", "yc")),
        P(),
    )
    return jax.shard_map(
        per_device_body, mesh=fine, in_specs=placed, out_specs=P(("x", "yc", "head"), None), check_vma=False
    )
```
